128 devices in a mesh: req: 16 (over y, z), mp: 8 (over x, core).
Axes of the slice: x: 4, y: 4, z: 4, core: 2. Of those that a mesh axis runs over, the one named last changes fastest.
Arguments:
- hidden_in: bfloat16 [16384, 2048], P('req', 'mp'), may hold values from -6 to 6
- w_qkv: bfloat16 [3, 2048, 2048], P(None, 'req', 'mp'), may hold values from -0.125 to 0.125
- w_out: bfloat16 [2048, 2048], P('mp', 'req'), may hold values from -0.125 to 0.125
- attn_gain: bfloat16 [2048], replicated, may hold values from 0.099609375 to 1.8984375
- mlp_gain: bfloat16 [2048], replicated, may hold values from 0.099609375 to 1.8984375
- w_gate: bfloat16 [2048, 8192], P('req', 'mp'), may hold values from -0.125 to 0.125
- w_up: bfloat16 [2048, 8192], P('req', 'mp'), may hold values from -0.125 to 0.125
- w_down: bfloat16 [8192, 2048], P('mp', 'req'), may hold values from -0.0625 to 0.0625
- k_cache: bfloat16 [16, 4096, 2048], P('req', None, 'mp'), may hold values from -363 to 363
- v_cache: bfloat16 [16, 4096, 2048], P('req', None, 'mp'), may hold values from -6 to 6
- cache_len: int32 [16], P('req'), may hold values from 256 to 4096, as said below
Outputs:
- hidden_out: bfloat16 [16384, 2048], P('req', 'mp')
- new_keys: bfloat16 [16384, 2048], P('req', 'mp')
- new_values: bfloat16 [16384, 2048], P('req', 'mp')
The draws below stay inside these ranges and needn't reach their ends.
Inputs may be any that keep to these rules, and one draw needn't show every extreme that they name: Each request uses its first cache_len slots; later slots hold unused data. Some request's cache is full in every draw.
All inputs are finite; a program needn't handle non-finite values.
Results may differ from the reference program's by a relative error of at most 0.02.
Values may be sent and summed in bfloat16 or wider, within the bound.
No kernel may reach another device: no remote copies, remote signals or barrier semaphores. Data moves between devices by JAX's collectives and lax.ppermute only.
A program may use at most 128 MiB of HBM per device.

```python
import jax
import jax.numpy as jnp
from jax import lax

D = 2048
HEADS = 32
HD = 64
FF = 8192
NEW = 1024
CACHE = 4096
REQUESTS = 16
TOKENS = 16384
N_MP = 8


def draw_cache_len(key, part):
    first, second = jax.random.split(jax.random.fold_in(key, 17))
    drawn = jax.random.randint(first, (REQUESTS,), CACHE // 16, CACHE + 1, dtype=jnp.int32)
    chosen = jax.random.randint(second, (), 0, REQUESTS, dtype=jnp.int32)
    return jnp.where(jnp.arange(REQUESTS, dtype=jnp.int32) == chosen, CACHE, drawn).astype(jnp.int32)


def draw_k_cache(key, part):
    noise_key = jax.random.fold_in(jax.random.fold_in(key, 29), 0)
    noise = jnp.clip(jax.random.normal(noise_key, (REQUESTS, CACHE, D), jnp.float32), -6.0, 6.0)
    return noise.astype(jnp.bfloat16)


def steps_of(stream_key, extent, cuts, smallest, largest):
    level, own = 1.0, jax.random.fold_in(stream_key, 6)
    for position, parts in cuts:
        steps = jnp.exp(jax.random.uniform(jax.random.fold_in(own, position), (parts,), jnp.float32, smallest / len(cuts), largest / len(cuts)))
        level = level * jnp.repeat(steps, extent[position] // parts).reshape([-1 if axis == position else 1 for axis in range(len(extent))])
    return level


def scatter_about(own_key, shape, scale, limit, pieces=(), kind=jnp.bfloat16):
    array = scale * jax.random.normal(own_key, shape, jnp.float32)
    if pieces:
        array = array * steps_of(own_key, shape, pieces, -0.22, 0.18)
    return jnp.clip(array, -limit, limit).astype(kind)


def setup_inputs(seed: int = 0) -> dict:
    keys = jax.random.split(jax.random.key(seed), 12)
    hidden_in = scatter_about(keys[0], (TOKENS, D), 1.0, 6.0, ((0, 16), (1, 8)))
    w_qkv = scatter_about(keys[1], (3, D, D), D ** -0.5, 0.125, ((1, 16), (2, 8)))
    w_out = scatter_about(keys[2], (D, D), D ** -0.5, 0.125, ((0, 8), (1, 16)))
    attn_gain = jnp.clip(1.0 + 0.18 * jax.random.normal(keys[3], (D,), jnp.float32), 0.099609375, 1.8984375).astype(jnp.bfloat16)
    mlp_gain = jnp.clip(1.0 + 0.18 * jax.random.normal(keys[4], (D,), jnp.float32), 0.099609375, 1.8984375).astype(jnp.bfloat16)
    w_gate = scatter_about(keys[5], (D, FF), D ** -0.5, 0.125, ((0, 16), (1, 8)))
    w_up = scatter_about(keys[6], (D, FF), D ** -0.5, 0.125, ((0, 16), (1, 8)))
    w_down = scatter_about(keys[7], (FF, D), FF ** -0.5, 0.0625, ((0, 8), (1, 16)))
    k_cache = draw_k_cache(jax.random.fold_in(keys[11], 71), 0)
    v_cache = scatter_about(keys[9], (REQUESTS, CACHE, D), 1.0, 6.0, ((0, 16), (2, 8)))
    cache_len = draw_cache_len(jax.random.fold_in(keys[11], 71), 0)
    return {"hidden_in": hidden_in, "w_qkv": w_qkv, "w_out": w_out, "attn_gain": attn_gain, "mlp_gain": mlp_gain, "w_gate": w_gate, "w_up": w_up, "w_down": w_down, "k_cache": k_cache, "v_cache": v_cache, "cache_len": cache_len}


THETA = 130000.0
EPSILON = 1e-05

def rms_scale(rows, gain):
    values = rows.astype(jnp.float32)
    meansq = lax.optimization_barrier(jnp.mean(values * values, axis=-1, keepdims=True))
    return (values * lax.rsqrt(meansq + EPSILON) * gain.astype(jnp.float32)).astype(jnp.bfloat16)

def rotate(tensor, positions):
    half = tensor.shape[-1] // 2
    freq = THETA ** (-(jnp.arange(half, dtype=jnp.float32) * 2.0 / tensor.shape[-1]))
    angle = positions[:, None, None] * freq[None, None, :]
    cosine = jnp.cos(angle)
    sine = jnp.sin(angle)
    first = tensor[..., :half]
    second = tensor[..., half:]
    return jnp.concatenate([first * cosine - second * sine, second * cosine + first * sine], axis=-1)

def grouped_sum(left, right, groups):
    width = left.shape[1] // groups
    total = jnp.zeros((left.shape[0], right.shape[1]), jnp.float32)
    for group in range(groups):
        part = jnp.dot(left[:, group * width:(group + 1) * width], right[group * width:(group + 1) * width], preferred_element_type=jnp.float32).astype(jnp.bfloat16)
        part = lax.optimization_barrier(part)
        total = total + part.astype(jnp.float32)
    return total

def reference(hidden_in, w_qkv, w_out, attn_gain, mlp_gain, w_gate, w_up, w_down, k_cache, v_cache, cache_len):
    scale = HD ** (-0.5)
    normed = rms_scale(hidden_in, attn_gain)
    proj_query = jnp.dot(normed, w_qkv[0], preferred_element_type=jnp.float32)
    proj_key = jnp.dot(normed, w_qkv[1], preferred_element_type=jnp.float32)
    proj_value = jnp.dot(normed, w_qkv[2], preferred_element_type=jnp.float32)
    offsets = jnp.repeat(cache_len.astype(jnp.int32), NEW) + jnp.tile(jnp.arange(NEW, dtype=jnp.int32), REQUESTS)
    positions = offsets.astype(jnp.float32)
    queries = rotate(proj_query.reshape(TOKENS, HEADS, HD), positions).astype(jnp.bfloat16)
    new_keys = rotate(proj_key.reshape(TOKENS, HEADS, HD), positions).astype(jnp.bfloat16)
    new_values = proj_value.astype(jnp.bfloat16).reshape(TOKENS, HEADS, HD)

    def one_request(inputs):
        req_q, req_k, req_v, cache_k, cache_v, length = inputs
        slot_ok = jnp.arange(CACHE, dtype=jnp.int32) < length
        rows = jnp.arange(NEW, dtype=jnp.int32)
        causal = rows[:, None] >= rows[None, :]
        mask = jnp.concatenate([jnp.broadcast_to(slot_ok[None, :], (NEW, CACHE)), causal], axis=1)

        def one_head(head_in):
            head_q, head_k, head_v, head_ck, head_cv = head_in
            score_c = jnp.dot(head_q, head_ck.T, preferred_element_type=jnp.float32) * scale
            score_n = jnp.dot(head_q, head_k.T, preferred_element_type=jnp.float32) * scale
            scores = jnp.where(mask, jnp.concatenate([score_c, score_n], axis=1), -1e+30)
            top = lax.optimization_barrier(jnp.max(scores, axis=1, keepdims=True))
            probs = jnp.where(mask, jnp.exp(scores - top), 0.0)
            total = lax.optimization_barrier(jnp.sum(probs, axis=1, keepdims=True))
            values = jnp.concatenate([head_cv, head_v], axis=0)
            weighted = jnp.dot(probs.astype(jnp.bfloat16), values, preferred_element_type=jnp.float32)
            return weighted / total
        per_head = lax.map(one_head, (req_q.transpose(1, 0, 2), req_k.transpose(1, 0, 2), req_v.transpose(1, 0, 2), cache_k.transpose(1, 0, 2), cache_v.transpose(1, 0, 2)))
        return per_head.transpose(1, 0, 2).reshape(NEW, D).astype(jnp.bfloat16)
    attn = lax.map(one_request, (queries.reshape(REQUESTS, NEW, HEADS, HD), new_keys.reshape(REQUESTS, NEW, HEADS, HD), new_values.reshape(REQUESTS, NEW, HEADS, HD), k_cache.reshape(REQUESTS, CACHE, HEADS, HD), v_cache.reshape(REQUESTS, CACHE, HEADS, HD), cache_len.astype(jnp.int32)))
    attn = attn.reshape(TOKENS, D)
    mid = (hidden_in.astype(jnp.float32) + grouped_sum(attn, w_out, N_MP)).astype(jnp.bfloat16)
    normed2 = rms_scale(mid, mlp_gain)
    gate = jnp.dot(normed2, w_gate, preferred_element_type=jnp.float32)
    upper = jnp.dot(normed2, w_up, preferred_element_type=jnp.float32)
    units = (jax.nn.silu(gate) * upper).astype(jnp.bfloat16)
    hidden_out = (mid.astype(jnp.float32) + grouped_sum(units, w_down, N_MP)).astype(jnp.bfloat16)
    return (hidden_out, new_keys.reshape(TOKENS, D), new_values.reshape(TOKENS, D))
```

```python
import jax
import jax.numpy as jnp
from jax import lax
from jax.sharding import PartitionSpec as P

HD = 64


THETA = 130000.0
EPSILON = 1e-05
NEG_FILL = -1e30


def rms_scale(rows, gain):
    values = rows.astype(jnp.float32)
    meansq = jnp.mean(values * values, axis=-1, keepdims=True)
    return (values * lax.rsqrt(meansq + EPSILON) * gain.astype(jnp.float32)).astype(jnp.bfloat16)


def rotate(tensor, positions):
    half = tensor.shape[-1] // 2
    freq = THETA ** (-(jnp.arange(half, dtype=jnp.float32) * 2.0 / tensor.shape[-1]))
    angle = positions[:, None, None] * freq[None, None, :]
    cosine = jnp.cos(angle)
    sine = jnp.sin(angle)
    first = tensor[..., :half]
    second = tensor[..., half:]
    return jnp.concatenate(
        [first * cosine - second * sine, second * cosine + first * sine], axis=-1
    )


def _side(n):
    side = int(round(n ** 0.5))
    return side if side * side == n else 1


def gather_req(block, axis, n_req):
    side_z = _side(n_req)
    side_y = n_req // side_z
    me = lax.axis_index("req")
    row, col = me // side_z, me % side_z

    def shift_z(k):
        return [(s, (s // side_z) * side_z + (s % side_z - k) % side_z) for s in range(n_req)]

    def shift_y(k):
        return [(s, ((s // side_z - k) % side_y) * side_z + s % side_z) for s in range(n_req)]

    parts = [block] + [lax.ppermute(block, "req", shift_z(k)) for k in range(1, side_z)]
    stage = jnp.stack(parts, axis=axis)
    parts = [stage] + [lax.ppermute(stage, "req", shift_y(k)) for k in range(1, side_y)]
    full = jnp.stack(parts, axis=axis)
    full = jnp.roll(full, (row, col), axis=(axis, axis + 1))
    shape = list(block.shape)
    shape[axis] *= n_req
    return full.reshape(shape)


def absorb(carry, queries, keys, values, valid):
    top, total, accum = carry
    scores = jnp.einsum("qhd,khd->hqk", queries, keys, preferred_element_type=jnp.float32) * HD ** (
        -0.5
    )
    scores = jnp.where(valid[None], scores, NEG_FILL)
    new_top = jnp.maximum(top, jnp.max(scores, axis=-1, keepdims=True))
    factor = jnp.exp(top - new_top)
    probs = jnp.where(valid[None], jnp.exp(scores - new_top), 0.0)
    total = total * factor + jnp.sum(probs, axis=-1, keepdims=True)
    accum = accum * factor + jnp.einsum(
        "hqk,khd->hqd", probs.astype(jnp.bfloat16), values, preferred_element_type=jnp.float32
    )
    return (new_top, total, accum)


def on_device(
    hidden_in, w_qkv, w_out, attn_gain, mlp_gain, w_gate, w_up, w_down, k_cache, v_cache, cache_len
):
    new_count = hidden_in.shape[0]
    n_req = lax.axis_size("req")
    w_qkv_full = gather_req(w_qkv, 1, n_req)
    out_rows = w_out.shape[0]
    out_down = gather_req(jnp.concatenate([w_out, w_down], axis=0), 1, n_req)
    w_out_full, w_down_full = out_down[:out_rows], out_down[out_rows:]
    gate_up = gather_req(jnp.stack([w_gate, w_up]), 1, n_req)
    width = w_qkv.shape[2]
    heads_local = width // HD
    slots = k_cache.shape[1]
    full_rows = lax.all_gather(hidden_in, "mp", axis=1, tiled=True)
    normed = rms_scale(full_rows, attn_gain)
    columns = normed
    projected = jnp.einsum(
        "nd,kdw->knw",
        columns,
        w_qkv_full,
        preferred_element_type=jnp.float32,
    )
    length = cache_len[0]
    positions = (length + jnp.arange(new_count, dtype=jnp.int32)).astype(jnp.float32)
    queries = rotate(projected[0].reshape(new_count, heads_local, HD), positions).astype(
        jnp.bfloat16
    )
    fresh_keys = rotate(projected[1].reshape(new_count, heads_local, HD), positions).astype(
        jnp.bfloat16
    )
    fresh_values = projected[2].astype(jnp.bfloat16).reshape(new_count, heads_local, HD)
    rows = jnp.arange(new_count, dtype=jnp.int32)
    causal = rows[:, None] >= rows[None, :]
    start_carry = (
        jnp.full((heads_local, new_count, 1), NEG_FILL, jnp.float32),
        jnp.zeros((heads_local, new_count, 1), jnp.float32),
        jnp.zeros((heads_local, new_count, HD), jnp.float32),
    )
    carry = absorb(start_carry, queries, fresh_keys, fresh_values, causal)
    cache_keys = k_cache[0].reshape(slots, heads_local, HD)
    cache_values = v_cache[0].reshape(slots, heads_local, HD)
    block = min(slots, 512)
    count = (length + block - 1) // block

    def step_block(index, state):
        begin = index * block
        keys = lax.dynamic_slice_in_dim(cache_keys, begin, block, 0)
        values = lax.dynamic_slice_in_dim(cache_values, begin, block, 0)
        valid = (begin + jnp.arange(block, dtype=jnp.int32) < length)[None, :]
        return absorb(state, queries, keys, values, valid)

    top, total, accum = lax.fori_loop(0, count, step_block, carry)
    attn = (accum / total).transpose(1, 0, 2).reshape(new_count, width).astype(jnp.bfloat16)
    partial_value = jnp.dot(
        attn, w_out_full, preferred_element_type=jnp.float32
    )
    summed = lax.psum_scatter(
        partial_value.astype(jnp.bfloat16), "mp", scatter_dimension=1, tiled=True
    ).astype(jnp.float32)
    mid_local = (hidden_in.astype(jnp.float32) + summed).astype(jnp.bfloat16)
    mid_full = lax.all_gather(mid_local, "mp", axis=1, tiled=True)
    normed2 = rms_scale(mid_full, mlp_gain)
    columns = normed2
    gate = jnp.dot(
        columns,
        gate_up[0],
        preferred_element_type=jnp.float32,
    )
    upper = jnp.dot(
        columns, gate_up[1], preferred_element_type=jnp.float32
    )
    units = (jax.nn.silu(gate) * upper).astype(jnp.bfloat16)
    terms = jnp.dot(
        units, w_down_full, preferred_element_type=jnp.float32
    )
    reduced = lax.psum_scatter(
        terms.astype(jnp.bfloat16), "mp", scatter_dimension=1, tiled=True
    ).astype(jnp.float32)
    hidden_out = (mid_local.astype(jnp.float32) + reduced).astype(jnp.bfloat16)
    return (
        hidden_out,
        fresh_keys.reshape(new_count, width),
        fresh_values.reshape(new_count, width),
    )


def solution(mesh):
    return jax.shard_map(
        on_device,
        mesh=mesh,
        in_specs=(
            P("req", "mp"),
            P(None, "req", "mp"),
            P("mp", "req"),
            P(),
            P(),
            P("req", "mp"),
            P("req", "mp"),
            P("mp", "req"),
            P("req", None, "mp"),
            P("req", None, "mp"),
            P("req"),
        ),
        out_specs=(P("req", "mp"), P("req", "mp"), P("req", "mp")),
        check_vma=False,
    )
```

```python
import jax
import jax.numpy as jnp
from jax import lax
from jax.sharding import PartitionSpec as P

HD = 64


THETA = 130000.0
EPSILON = 1e-05
NEG_FILL = -1e30


def rms_scale(rows, gain):
    values = rows.astype(jnp.float32)
    meansq = jnp.mean(values * values, axis=-1, keepdims=True)
    return (values * lax.rsqrt(meansq + EPSILON) * gain.astype(jnp.float32)).astype(jnp.bfloat16)


def rotate(tensor, positions):
    half = tensor.shape[-1] // 2
    freq = THETA ** (-(jnp.arange(half, dtype=jnp.float32) * 2.0 / tensor.shape[-1]))
    angle = positions[:, None, None] * freq[None, None, :]
    cosine = jnp.cos(angle)
    sine = jnp.sin(angle)
    first = tensor[..., :half]
    second = tensor[..., half:]
    return jnp.concatenate(
        [first * cosine - second * sine, second * cosine + first * sine], axis=-1
    )


def gather_packed(blocks, axes, axis_name):
    count = lax.axis_size(axis_name)
    joined = jnp.concatenate([block.reshape(-1) for block in blocks])
    gathered = lax.all_gather(joined, axis_name, axis=0, tiled=False)
    outs = []
    offset = 0
    for block, axis in zip(blocks, axes):
        size = block.size
        piece = gathered[:, offset:offset + size].reshape((count,) + block.shape)
        piece = jnp.moveaxis(piece, 0, axis)
        shape = list(block.shape)
        shape[axis] *= count
        outs.append(piece.reshape(shape))
        offset += size
    return outs


def absorb(carry, queries, keys, values, valid):
    top, total, accum = carry
    scores = jnp.einsum("qhd,khd->hqk", queries, keys, preferred_element_type=jnp.float32) * HD ** (
        -0.5
    )
    scores = jnp.where(valid[None], scores, NEG_FILL)
    new_top = jnp.maximum(top, jnp.max(scores, axis=-1, keepdims=True))
    factor = jnp.exp(top - new_top)
    probs = jnp.where(valid[None], jnp.exp(scores - new_top), 0.0)
    total = total * factor + jnp.sum(probs, axis=-1, keepdims=True)
    accum = accum * factor + jnp.einsum(
        "hqk,khd->hqd", probs.astype(jnp.bfloat16), values, preferred_element_type=jnp.float32
    )
    return (new_top, total, accum)


def on_device(
    hidden_in, w_qkv, w_out, attn_gain, mlp_gain, w_gate, w_up, w_down, k_cache, v_cache, cache_len
):
    new_count = hidden_in.shape[0]
    w_qkv_full = lax.all_gather(w_qkv, "req", axis=1, tiled=True)
    w_gate_full, w_up_full, w_down_full, w_out_full = gather_packed(
        [w_gate, w_up, w_down, w_out], [0, 0, 1, 1], "req"
    )
    width = w_qkv.shape[2]
    heads_local = width // HD
    slots = k_cache.shape[1]
    full_rows = lax.all_gather(hidden_in, "mp", axis=1, tiled=True)
    normed = rms_scale(full_rows, attn_gain)
    columns = normed
    projected = jnp.einsum(
        "nd,kdw->knw",
        columns,
        w_qkv_full,
        preferred_element_type=jnp.float32,
    )
    length = cache_len[0]
    positions = (length + jnp.arange(new_count, dtype=jnp.int32)).astype(jnp.float32)
    queries = rotate(projected[0].reshape(new_count, heads_local, HD), positions).astype(
        jnp.bfloat16
    )
    fresh_keys = rotate(projected[1].reshape(new_count, heads_local, HD), positions).astype(
        jnp.bfloat16
    )
    fresh_values = projected[2].astype(jnp.bfloat16).reshape(new_count, heads_local, HD)
    rows = jnp.arange(new_count, dtype=jnp.int32)
    causal = rows[:, None] >= rows[None, :]
    start_carry = (
        jnp.full((heads_local, new_count, 1), NEG_FILL, jnp.float32),
        jnp.zeros((heads_local, new_count, 1), jnp.float32),
        jnp.zeros((heads_local, new_count, HD), jnp.float32),
    )
    carry = absorb(start_carry, queries, fresh_keys, fresh_values, causal)
    cache_keys = k_cache[0].reshape(slots, heads_local, HD)
    cache_values = v_cache[0].reshape(slots, heads_local, HD)
    block = min(slots, 512)
    count = (length + block - 1) // block

    def step_block(index, state):
        begin = index * block
        keys = lax.dynamic_slice_in_dim(cache_keys, begin, block, 0)
        values = lax.dynamic_slice_in_dim(cache_values, begin, block, 0)
        valid = (begin + jnp.arange(block, dtype=jnp.int32) < length)[None, :]
        return absorb(state, queries, keys, values, valid)

    top, total, accum = lax.fori_loop(0, count, step_block, carry)
    attn = (accum / total).transpose(1, 0, 2).reshape(new_count, width).astype(jnp.bfloat16)
    partial_value = jnp.dot(
        attn, w_out_full, preferred_element_type=jnp.float32
    )
    summed = lax.psum(partial_value.astype(jnp.bfloat16), "mp").astype(jnp.float32)
    mid_full = (full_rows.astype(jnp.float32) + summed).astype(jnp.bfloat16)
    own = hidden_in.shape[1]
    mid_local = lax.dynamic_slice_in_dim(mid_full, lax.axis_index("mp") * own, own, axis=1)
    normed2 = rms_scale(mid_full, mlp_gain)
    columns = normed2
    gate = jnp.dot(
        columns,
        w_gate_full,
        preferred_element_type=jnp.float32,
    )
    upper = jnp.dot(
        columns, w_up_full, preferred_element_type=jnp.float32
    )
    units = (jax.nn.silu(gate) * upper).astype(jnp.bfloat16)
    terms = jnp.dot(
        units, w_down_full, preferred_element_type=jnp.float32
    )
    reduced = lax.psum_scatter(
        terms.astype(jnp.bfloat16), "mp", scatter_dimension=1, tiled=True
    ).astype(jnp.float32)
    hidden_out = (mid_local.astype(jnp.float32) + reduced).astype(jnp.bfloat16)
    return (
        hidden_out,
        fresh_keys.reshape(new_count, width),
        fresh_values.reshape(new_count, width),
    )


def solution(mesh):
    return jax.shard_map(
        on_device,
        mesh=mesh,
        in_specs=(
            P("req", "mp"),
            P(None, "req", "mp"),
            P("mp", "req"),
            P(),
            P(),
            P("req", "mp"),
            P("req", "mp"),
            P("mp", "req"),
            P("req", None, "mp"),
            P("req", None, "mp"),
            P("req"),
        ),
        out_specs=(P("req", "mp"), P("req", "mp"), P("req", "mp")),
        check_vma=False,
    )
```

```python
import jax
import jax.numpy as jnp
from jax import lax
from jax.sharding import PartitionSpec as P

HD = 64


THETA = 130000.0
EPSILON = 1e-05
NEG_FILL = -1e30


def rms_scale(rows, gain):
    values = rows.astype(jnp.float32)
    meansq = jnp.mean(values * values, axis=-1, keepdims=True)
    return (values * lax.rsqrt(meansq + EPSILON) * gain.astype(jnp.float32)).astype(jnp.bfloat16)


def rotate(tensor, positions):
    half = tensor.shape[-1] // 2
    freq = THETA ** (-(jnp.arange(half, dtype=jnp.float32) * 2.0 / tensor.shape[-1]))
    angle = positions[:, None, None] * freq[None, None, :]
    cosine = jnp.cos(angle)
    sine = jnp.sin(angle)
    first = tensor[..., :half]
    second = tensor[..., half:]
    return jnp.concatenate(
        [first * cosine - second * sine, second * cosine + first * sine], axis=-1
    )


def gather_packed(blocks, axes, axis_name):
    count = lax.axis_size(axis_name)
    lane = 128
    joined = jnp.concatenate([block.reshape(-1, lane) for block in blocks], axis=0)
    gathered = lax.all_gather(joined, axis_name, axis=0, tiled=False)
    outs = []
    offset = 0
    for block, axis in zip(blocks, axes):
        rows = block.size // lane
        piece = gathered[:, offset:offset + rows].reshape((count,) + block.shape)
        piece = jnp.moveaxis(piece, 0, axis)
        shape = list(block.shape)
        shape[axis] *= count
        outs.append(piece.reshape(shape))
        offset += rows
    return outs


def absorb(carry, queries, keys, values, valid):
    top, total, accum = carry
    scores = jnp.einsum("qhd,khd->hqk", queries, keys, preferred_element_type=jnp.float32) * HD ** (
        -0.5
    )
    scores = jnp.where(valid[None], scores, NEG_FILL)
    new_top = jnp.maximum(top, jnp.max(scores, axis=-1, keepdims=True))
    factor = jnp.exp(top - new_top)
    probs = jnp.where(valid[None], jnp.exp(scores - new_top), 0.0)
    total = total * factor + jnp.sum(probs, axis=-1, keepdims=True)
    accum = accum * factor + jnp.einsum(
        "hqk,khd->hqd", probs.astype(jnp.bfloat16), values, preferred_element_type=jnp.float32
    )
    return (new_top, total, accum)


def on_device(
    hidden_in, w_qkv, w_out, attn_gain, mlp_gain, w_gate, w_up, w_down, k_cache, v_cache, cache_len
):
    new_count = hidden_in.shape[0]
    w_qkv_full = lax.all_gather(w_qkv, "req", axis=1, tiled=True)
    w_gate_full, w_up_full, w_down_full, w_out_full = gather_packed(
        [w_gate, w_up, w_down, w_out], [0, 0, 1, 1], "req"
    )
    width = w_qkv.shape[2]
    heads_local = width // HD
    slots = k_cache.shape[1]
    full_rows = lax.all_gather(hidden_in, "mp", axis=1, tiled=True)
    normed = rms_scale(full_rows, attn_gain)
    columns = normed
    projected = jnp.einsum(
        "nd,kdw->knw",
        columns,
        w_qkv_full,
        preferred_element_type=jnp.float32,
    )
    length = cache_len[0]
    positions = (length + jnp.arange(new_count, dtype=jnp.int32)).astype(jnp.float32)
    queries = rotate(projected[0].reshape(new_count, heads_local, HD), positions).astype(
        jnp.bfloat16
    )
    fresh_keys = rotate(projected[1].reshape(new_count, heads_local, HD), positions).astype(
        jnp.bfloat16
    )
    fresh_values = projected[2].astype(jnp.bfloat16).reshape(new_count, heads_local, HD)
    rows = jnp.arange(new_count, dtype=jnp.int32)
    causal = rows[:, None] >= rows[None, :]
    start_carry = (
        jnp.full((heads_local, new_count, 1), NEG_FILL, jnp.float32),
        jnp.zeros((heads_local, new_count, 1), jnp.float32),
        jnp.zeros((heads_local, new_count, HD), jnp.float32),
    )
    carry = absorb(start_carry, queries, fresh_keys, fresh_values, causal)
    cache_keys = k_cache[0].reshape(slots, heads_local, HD)
    cache_values = v_cache[0].reshape(slots, heads_local, HD)
    block = min(slots, 512)
    count = (length + block - 1) // block

    def step_block(index, state):
        begin = index * block
        keys = lax.dynamic_slice_in_dim(cache_keys, begin, block, 0)
        values = lax.dynamic_slice_in_dim(cache_values, begin, block, 0)
        valid = (begin + jnp.arange(block, dtype=jnp.int32) < length)[None, :]
        return absorb(state, queries, keys, values, valid)

    top, total, accum = lax.fori_loop(0, count, step_block, carry)
    attn = (accum / total).transpose(1, 0, 2).reshape(new_count, width).astype(jnp.bfloat16)
    partial_value = jnp.dot(
        attn, w_out_full, preferred_element_type=jnp.float32
    )
    summed = lax.psum(partial_value.astype(jnp.bfloat16), "mp").astype(jnp.float32)
    mid_full = (full_rows.astype(jnp.float32) + summed).astype(jnp.bfloat16)
    own = hidden_in.shape[1]
    mid_local = lax.dynamic_slice_in_dim(mid_full, lax.axis_index("mp") * own, own, axis=1)
    normed2 = rms_scale(mid_full, mlp_gain)
    columns = normed2
    gate = jnp.dot(
        columns,
        w_gate_full,
        preferred_element_type=jnp.float32,
    )
    upper = jnp.dot(
        columns, w_up_full, preferred_element_type=jnp.float32
    )
    units = (jax.nn.silu(gate) * upper).astype(jnp.bfloat16)
    terms = jnp.dot(
        units, w_down_full, preferred_element_type=jnp.float32
    )
    reduced = lax.psum_scatter(
        terms.astype(jnp.bfloat16), "mp", scatter_dimension=1, tiled=True
    ).astype(jnp.float32)
    hidden_out = (mid_local.astype(jnp.float32) + reduced).astype(jnp.bfloat16)
    return (
        hidden_out,
        fresh_keys.reshape(new_count, width),
        fresh_values.reshape(new_count, width),
    )


def solution(mesh):
    return jax.shard_map(
        on_device,
        mesh=mesh,
        in_specs=(
            P("req", "mp"),
            P(None, "req", "mp"),
            P("mp", "req"),
            P(),
            P(),
            P("req", "mp"),
            P("req", "mp"),
            P("mp", "req"),
            P("req", None, "mp"),
            P("req", None, "mp"),
            P("req"),
        ),
        out_specs=(P("req", "mp"), P("req", "mp"), P("req", "mp")),
        check_vma=False,
    )
```

```python
import jax
import jax.numpy as jnp
from jax import lax
from jax.sharding import PartitionSpec as P
from jax.experimental import pallas as pl
from jax.experimental.pallas import tpu as pltpu
import functools

HD = 64


THETA = 130000.0
EPSILON = 1e-05
NEG_FILL = -1e30


def rms_scale(rows, gain):
    values = rows.astype(jnp.float32)
    meansq = jnp.mean(values * values, axis=-1, keepdims=True)
    return (values * lax.rsqrt(meansq + EPSILON) * gain.astype(jnp.float32)).astype(jnp.bfloat16)


def rotate(tensor, positions):
    half = tensor.shape[-1] // 2
    freq = THETA ** (-(jnp.arange(half, dtype=jnp.float32) * 2.0 / tensor.shape[-1]))
    angle = positions[:, None, None] * freq[None, None, :]
    cosine = jnp.cos(angle)
    sine = jnp.sin(angle)
    first = tensor[..., :half]
    second = tensor[..., half:]
    return jnp.concatenate(
        [first * cosine - second * sine, second * cosine + first * sine], axis=-1
    )


def gather_packed(blocks, axes, axis_name):
    count = lax.axis_size(axis_name)
    lane = 128
    joined = jnp.concatenate([block.reshape(-1, lane) for block in blocks], axis=0)
    gathered = lax.all_gather(joined, axis_name, axis=0, tiled=False)
    outs = []
    offset = 0
    for block, axis in zip(blocks, axes):
        rows = block.size // lane
        piece = gathered[:, offset:offset + rows].reshape((count,) + block.shape)
        piece = jnp.moveaxis(piece, 0, axis)
        shape = list(block.shape)
        shape[axis] *= count
        outs.append(piece.reshape(shape))
        offset += rows
    return outs


def flash_body(len_ref, q_ref, kc_ref, vc_ref, kn_ref, vn_ref, o_ref, m_sc, l_sc, acc_sc, *, tk, n_cache, scale):
    j = pl.program_id(1)
    length = len_ref[0]
    tq = q_ref.shape[1]

    @pl.when(j == 0)
    def _():
        m_sc[...] = jnp.full(m_sc.shape, NEG_FILL, jnp.float32)
        l_sc[...] = jnp.zeros(l_sc.shape, jnp.float32)
        acc_sc[...] = jnp.zeros(acc_sc.shape, jnp.float32)

    def update(k, v, mask):
        s = lax.dot_general(q_ref[0], k, (((1,), (1,)), ((), ())), preferred_element_type=jnp.float32) * scale
        if mask is not None:
            s = jnp.where(mask, s, NEG_FILL)
        m_prev = m_sc[...]
        m_new = jnp.maximum(m_prev, jnp.max(s, axis=1, keepdims=True))
        alpha = jnp.exp(m_prev - m_new)
        p = jnp.exp(s - m_new)
        if mask is not None:
            p = jnp.where(mask, p, 0.0)
        l_sc[...] = alpha * l_sc[...] + jnp.sum(p, axis=1, keepdims=True)
        acc_sc[...] = alpha * acc_sc[...] + jnp.dot(p.astype(jnp.bfloat16), v, preferred_element_type=jnp.float32)
        m_sc[...] = m_new

    begin = j * tk

    @pl.when((j < n_cache) & (begin + tk <= length))
    def _():
        update(kc_ref[0], vc_ref[0], None)

    @pl.when((j < n_cache) & (begin < length) & (begin + tk > length))
    def _():
        col = begin + lax.broadcasted_iota(jnp.int32, (tq, tk), 1)
        update(kc_ref[0], vc_ref[0], col < length)

    @pl.when(j == n_cache)
    def _():
        row = lax.broadcasted_iota(jnp.int32, (tq, tq), 0)
        col = lax.broadcasted_iota(jnp.int32, (tq, tq), 1)
        update(kn_ref[0], vn_ref[0], row >= col)
        o_ref[0] = (acc_sc[...] / l_sc[...]).astype(o_ref.dtype)


def flash_attention(length, q, kc, vc, kn, vn):
    heads, new_count, hd = q.shape
    slots = kc.shape[1]
    tk = min(new_count, slots)
    n_cache = slots // tk
    body = functools.partial(flash_body, tk=tk, n_cache=n_cache, scale=hd ** (-0.5))

    def cache_map(h, j, len_ref):
        last = jnp.maximum(len_ref[0] - 1, 0) // tk
        return (h, jnp.minimum(j, last), 0)

    fixed = lambda h, j, len_ref: (h, 0, 0)
    grid_spec = pltpu.PrefetchScalarGridSpec(
        num_scalar_prefetch=1,
        grid=(heads, n_cache + 1),
        in_specs=[
            pl.BlockSpec((1, new_count, hd), fixed),
            pl.BlockSpec((1, tk, hd), cache_map),
            pl.BlockSpec((1, tk, hd), cache_map),
            pl.BlockSpec((1, new_count, hd), fixed),
            pl.BlockSpec((1, new_count, hd), fixed),
        ],
        out_specs=pl.BlockSpec((1, new_count, hd), fixed),
        scratch_shapes=[
            pltpu.VMEM((new_count, 1), jnp.float32),
            pltpu.VMEM((new_count, 1), jnp.float32),
            pltpu.VMEM((new_count, hd), jnp.float32),
        ],
    )
    flops = 4 * heads * new_count * (slots + new_count) * hd
    cost = pl.CostEstimate(
        flops=flops,
        transcendentals=heads * new_count * (slots + new_count),
        bytes_accessed=2 * (q.size + kc.size + vc.size + kn.size + vn.size) + 4 * q.size,
    )
    return pl.pallas_call(
        body,
        grid_spec=grid_spec,
        out_shape=jax.ShapeDtypeStruct((heads, new_count, hd), jnp.bfloat16),
        compiler_params=pltpu.CompilerParams(
            dimension_semantics=("arbitrary", "arbitrary"), vmem_limit_bytes=56 * 1024 * 1024
        ),
        cost_estimate=cost,
    )(length, q, kc, vc, kn, vn)


def on_device(
    hidden_in, w_qkv, w_out, attn_gain, mlp_gain, w_gate, w_up, w_down, k_cache, v_cache, cache_len
):
    new_count = hidden_in.shape[0]
    w_qkv_full = lax.all_gather(w_qkv, "req", axis=1, tiled=True)
    w_gate_full, w_up_full, w_down_full, w_out_full = gather_packed(
        [w_gate, w_up, w_down, w_out], [0, 0, 1, 1], "req"
    )
    width = w_qkv.shape[2]
    heads_local = width // HD
    slots = k_cache.shape[1]
    full_rows = lax.all_gather(hidden_in, "mp", axis=1, tiled=True)
    normed = rms_scale(full_rows, attn_gain)
    columns = normed
    projected = jnp.einsum(
        "nd,kdw->knw",
        columns,
        w_qkv_full,
        preferred_element_type=jnp.float32,
    )
    length = cache_len[0]
    positions = (length + jnp.arange(new_count, dtype=jnp.int32)).astype(jnp.float32)
    queries = rotate(projected[0].reshape(new_count, heads_local, HD), positions).astype(
        jnp.bfloat16
    )
    fresh_keys = rotate(projected[1].reshape(new_count, heads_local, HD), positions).astype(
        jnp.bfloat16
    )
    fresh_values = projected[2].astype(jnp.bfloat16).reshape(new_count, heads_local, HD)
    head_major = lambda array: array.reshape(array.shape[0], heads_local, HD).transpose(1, 0, 2)
    attn_heads = flash_attention(
        cache_len,
        queries.transpose(1, 0, 2),
        head_major(k_cache[0]),
        head_major(v_cache[0]),
        fresh_keys.transpose(1, 0, 2),
        fresh_values.transpose(1, 0, 2),
    )
    attn = attn_heads.transpose(1, 0, 2).reshape(new_count, width)
    partial_value = jnp.dot(
        attn, w_out_full, preferred_element_type=jnp.float32
    )
    summed = lax.psum(partial_value.astype(jnp.bfloat16), "mp").astype(jnp.float32)
    mid_full = (full_rows.astype(jnp.float32) + summed).astype(jnp.bfloat16)
    own = hidden_in.shape[1]
    mid_local = lax.dynamic_slice_in_dim(mid_full, lax.axis_index("mp") * own, own, axis=1)
    normed2 = rms_scale(mid_full, mlp_gain)
    columns = normed2
    gate = jnp.dot(
        columns,
        w_gate_full,
        preferred_element_type=jnp.float32,
    )
    upper = jnp.dot(
        columns, w_up_full, preferred_element_type=jnp.float32
    )
    units = (jax.nn.silu(gate) * upper).astype(jnp.bfloat16)
    terms = jnp.dot(
        units, w_down_full, preferred_element_type=jnp.float32
    )
    reduced = lax.psum_scatter(
        terms.astype(jnp.bfloat16), "mp", scatter_dimension=1, tiled=True
    ).astype(jnp.float32)
    hidden_out = (mid_local.astype(jnp.float32) + reduced).astype(jnp.bfloat16)
    return (
        hidden_out,
        fresh_keys.reshape(new_count, width),
        fresh_values.reshape(new_count, width),
    )


def solution(mesh):
    return jax.shard_map(
        on_device,
        mesh=mesh,
        in_specs=(
            P("req", "mp"),
            P(None, "req", "mp"),
            P("mp", "req"),
            P(),
            P(),
            P("req", "mp"),
            P("req", "mp"),
            P("mp", "req"),
            P("req", None, "mp"),
            P("req", None, "mp"),
            P("req"),
        ),
        out_specs=(P("req", "mp"), P("req", "mp"), P("req", "mp")),
        check_vma=False,
    )
```

```python
import jax
import jax.numpy as jnp
from jax import lax
from jax.sharding import PartitionSpec as P
from jax.experimental import pallas as pl
from jax.experimental.pallas import tpu as pltpu
import functools

HD = 64


THETA = 130000.0
EPSILON = 1e-05
NEG_FILL = -1e30


def rms_scale(rows, gain):
    values = rows.astype(jnp.float32)
    meansq = jnp.mean(values * values, axis=-1, keepdims=True)
    return (values * lax.rsqrt(meansq + EPSILON) * gain.astype(jnp.float32)).astype(jnp.bfloat16)


def rotate(tensor, positions):
    half = tensor.shape[-1] // 2
    freq = THETA ** (-(jnp.arange(half, dtype=jnp.float32) * 2.0 / tensor.shape[-1]))
    angle = positions[:, None, None] * freq[None, None, :]
    cosine = jnp.cos(angle)
    sine = jnp.sin(angle)
    first = tensor[..., :half]
    second = tensor[..., half:]
    return jnp.concatenate(
        [first * cosine - second * sine, second * cosine + first * sine], axis=-1
    )


def gather_req_shifted(block, axis, axis_name):
    count = lax.axis_size(axis_name)
    side = int(round(count ** 0.5))
    me = lax.axis_index(axis_name)
    row, col = me // side, me % side

    def inner(k):
        return [(s, (s // side) * side + (s % side - k) % side) for s in range(count)]

    def outer(k):
        return [(s, ((s // side - k) % side) * side + s % side) for s in range(count)]

    parts = [block] + [lax.ppermute(block, axis_name, inner(k)) for k in range(1, side)]
    stage = jnp.stack(parts, axis=axis)
    parts = [stage] + [lax.ppermute(stage, axis_name, outer(k)) for k in range(1, side)]
    return jnp.stack(parts, axis=axis), row, col


def gather_packed(blocks, axes, axis_name):
    count = lax.axis_size(axis_name)
    lane = 128
    joined = jnp.concatenate([block.reshape(-1, lane) for block in blocks], axis=0)
    gathered = lax.all_gather(joined, axis_name, axis=0, tiled=False)
    outs = []
    offset = 0
    for block, axis in zip(blocks, axes):
        rows = block.size // lane
        piece = gathered[:, offset:offset + rows].reshape((count,) + block.shape)
        piece = jnp.moveaxis(piece, 0, axis)
        shape = list(block.shape)
        shape[axis] *= count
        outs.append(piece.reshape(shape))
        offset += rows
    return outs


def flash_body(len_ref, q_ref, kc_ref, vc_ref, kn_ref, vn_ref, o_ref, m_sc, l_sc, acc_sc, *, tk, n_cache, scale):
    j = pl.program_id(1)
    length = len_ref[0]
    tq = q_ref.shape[1]

    @pl.when(j == 0)
    def _():
        m_sc[...] = jnp.full(m_sc.shape, NEG_FILL, jnp.float32)
        l_sc[...] = jnp.zeros(l_sc.shape, jnp.float32)
        acc_sc[...] = jnp.zeros(acc_sc.shape, jnp.float32)

    def update(k, v, mask):
        s = lax.dot_general(q_ref[0], k, (((1,), (1,)), ((), ())), preferred_element_type=jnp.float32) * scale
        if mask is not None:
            s = jnp.where(mask, s, NEG_FILL)
        m_prev = m_sc[...]
        m_new = jnp.maximum(m_prev, jnp.max(s, axis=1, keepdims=True))
        alpha = jnp.exp(m_prev - m_new)
        p = jnp.exp(s - m_new)
        if mask is not None:
            p = jnp.where(mask, p, 0.0)
        l_sc[...] = alpha * l_sc[...] + jnp.sum(p, axis=1, keepdims=True)
        acc_sc[...] = alpha * acc_sc[...] + jnp.dot(p.astype(jnp.bfloat16), v, preferred_element_type=jnp.float32)
        m_sc[...] = m_new

    begin = j * tk

    @pl.when((j < n_cache) & (begin + tk <= length))
    def _():
        update(kc_ref[0], vc_ref[0], None)

    @pl.when((j < n_cache) & (begin < length) & (begin + tk > length))
    def _():
        col = begin + lax.broadcasted_iota(jnp.int32, (tq, tk), 1)
        update(kc_ref[0], vc_ref[0], col < length)

    @pl.when(j == n_cache)
    def _():
        row = lax.broadcasted_iota(jnp.int32, (tq, tq), 0)
        col = lax.broadcasted_iota(jnp.int32, (tq, tq), 1)
        update(kn_ref[0], vn_ref[0], row >= col)
        o_ref[0] = (acc_sc[...] / l_sc[...]).astype(o_ref.dtype)


def flash_attention(length, q, kc, vc, kn, vn):
    heads, new_count, hd = q.shape
    slots = kc.shape[1]
    tk = min(new_count, slots)
    n_cache = slots // tk
    body = functools.partial(flash_body, tk=tk, n_cache=n_cache, scale=hd ** (-0.5))

    def cache_map(h, j, len_ref):
        last = jnp.maximum(len_ref[0] - 1, 0) // tk
        return (h, jnp.minimum(j, last), 0)

    fixed = lambda h, j, len_ref: (h, 0, 0)
    grid_spec = pltpu.PrefetchScalarGridSpec(
        num_scalar_prefetch=1,
        grid=(heads, n_cache + 1),
        in_specs=[
            pl.BlockSpec((1, new_count, hd), fixed),
            pl.BlockSpec((1, tk, hd), cache_map),
            pl.BlockSpec((1, tk, hd), cache_map),
            pl.BlockSpec((1, new_count, hd), fixed),
            pl.BlockSpec((1, new_count, hd), fixed),
        ],
        out_specs=pl.BlockSpec((1, new_count, hd), fixed),
        scratch_shapes=[
            pltpu.VMEM((new_count, 1), jnp.float32),
            pltpu.VMEM((new_count, 1), jnp.float32),
            pltpu.VMEM((new_count, hd), jnp.float32),
        ],
    )
    flops = 4 * heads * new_count * (slots + new_count) * hd
    cost = pl.CostEstimate(
        flops=flops,
        transcendentals=heads * new_count * (slots + new_count),
        bytes_accessed=2 * (q.size + kc.size + vc.size + kn.size + vn.size) + 4 * q.size,
    )
    return pl.pallas_call(
        body,
        grid_spec=grid_spec,
        out_shape=jax.ShapeDtypeStruct((heads, new_count, hd), jnp.bfloat16),
        compiler_params=pltpu.CompilerParams(
            dimension_semantics=("arbitrary", "arbitrary"), vmem_limit_bytes=56 * 1024 * 1024
        ),
        cost_estimate=cost,
    )(length, q, kc, vc, kn, vn)


def on_device(
    hidden_in, w_qkv, w_out, attn_gain, mlp_gain, w_gate, w_up, w_down, k_cache, v_cache, cache_len
):
    new_count = hidden_in.shape[0]
    qkv_shifted, row, col = gather_req_shifted(w_qkv, 1, "req")
    side = qkv_shifted.shape[1]
    w_qkv_full = qkv_shifted.reshape(3, -1, w_qkv.shape[2])
    w_gate_full, w_up_full, w_down_full, w_out_full = gather_packed(
        [w_gate, w_up, w_down, w_out], [0, 0, 1, 1], "req"
    )
    width = w_qkv.shape[2]
    heads_local = width // HD
    slots = k_cache.shape[1]
    full_rows = lax.all_gather(hidden_in, "mp", axis=1, tiled=True)
    normed = rms_scale(full_rows, attn_gain)
    blocks = normed.reshape(new_count, side, side, -1)
    columns = jnp.roll(blocks, (-row, -col), axis=(1, 2)).reshape(new_count, -1)
    projected = jnp.einsum(
        "nd,kdw->knw",
        columns,
        w_qkv_full,
        preferred_element_type=jnp.float32,
    )
    length = cache_len[0]
    positions = (length + jnp.arange(new_count, dtype=jnp.int32)).astype(jnp.float32)
    queries = rotate(projected[0].reshape(new_count, heads_local, HD), positions).astype(
        jnp.bfloat16
    )
    fresh_keys = rotate(projected[1].reshape(new_count, heads_local, HD), positions).astype(
        jnp.bfloat16
    )
    fresh_values = projected[2].astype(jnp.bfloat16).reshape(new_count, heads_local, HD)
    head_major = lambda array: array.reshape(array.shape[0], heads_local, HD).transpose(1, 0, 2)
    attn_heads = flash_attention(
        cache_len,
        queries.transpose(1, 0, 2),
        head_major(k_cache[0]),
        head_major(v_cache[0]),
        fresh_keys.transpose(1, 0, 2),
        fresh_values.transpose(1, 0, 2),
    )
    attn = attn_heads.transpose(1, 0, 2).reshape(new_count, width)
    partial_value = jnp.dot(
        attn, w_out_full, preferred_element_type=jnp.float32
    )
    summed = lax.psum(partial_value.astype(jnp.bfloat16), "mp").astype(jnp.float32)
    mid_full = (full_rows.astype(jnp.float32) + summed).astype(jnp.bfloat16)
    own = hidden_in.shape[1]
    mid_local = lax.dynamic_slice_in_dim(mid_full, lax.axis_index("mp") * own, own, axis=1)
    normed2 = rms_scale(mid_full, mlp_gain)
    columns = normed2
    gate = jnp.dot(
        columns,
        w_gate_full,
        preferred_element_type=jnp.float32,
    )
    upper = jnp.dot(
        columns, w_up_full, preferred_element_type=jnp.float32
    )
    units = (jax.nn.silu(gate) * upper).astype(jnp.bfloat16)
    terms = jnp.dot(
        units, w_down_full, preferred_element_type=jnp.float32
    )
    reduced = lax.psum_scatter(
        terms.astype(jnp.bfloat16), "mp", scatter_dimension=1, tiled=True
    ).astype(jnp.float32)
    hidden_out = (mid_local.astype(jnp.float32) + reduced).astype(jnp.bfloat16)
    return (
        hidden_out,
        fresh_keys.reshape(new_count, width),
        fresh_values.reshape(new_count, width),
    )


def solution(mesh):
    return jax.shard_map(
        on_device,
        mesh=mesh,
        in_specs=(
            P("req", "mp"),
            P(None, "req", "mp"),
            P("mp", "req"),
            P(),
            P(),
            P("req", "mp"),
            P("req", "mp"),
            P("mp", "req"),
            P("req", None, "mp"),
            P("req", None, "mp"),
            P("req"),
        ),
        out_specs=(P("req", "mp"), P("req", "mp"), P("req", "mp")),
        check_vma=False,
    )
```

```python
import jax
import jax.numpy as jnp
from jax import lax
from jax.sharding import PartitionSpec as P
from jax.experimental import pallas as pl
from jax.experimental.pallas import tpu as pltpu
import functools

HD = 64


THETA = 130000.0
EPSILON = 1e-05
NEG_FILL = -1e30


def rms_scale(rows, gain):
    values = rows.astype(jnp.float32)
    meansq = jnp.mean(values * values, axis=-1, keepdims=True)
    return (values * lax.rsqrt(meansq + EPSILON) * gain.astype(jnp.float32)).astype(jnp.bfloat16)


def gather_req_shifted(block, axis, axis_name):
    count = lax.axis_size(axis_name)
    side = int(round(count ** 0.5))
    me = lax.axis_index(axis_name)
    row, col = me // side, me % side

    def inner(k):
        return [(s, (s // side) * side + (s % side - k) % side) for s in range(count)]

    def outer(k):
        return [(s, ((s // side - k) % side) * side + s % side) for s in range(count)]

    parts = [block] + [lax.ppermute(block, axis_name, inner(k)) for k in range(1, side)]
    stage = jnp.stack(parts, axis=axis)
    parts = [stage] + [lax.ppermute(stage, axis_name, outer(k)) for k in range(1, side)]
    return jnp.stack(parts, axis=axis), row, col


def gather_packed(blocks, axes, axis_name):
    count = lax.axis_size(axis_name)
    lane = 128
    joined = jnp.concatenate([block.reshape(-1, lane) for block in blocks], axis=0)
    gathered = lax.all_gather(joined, axis_name, axis=0, tiled=False)
    outs = []
    offset = 0
    for block, axis in zip(blocks, axes):
        rows = block.size // lane
        piece = gathered[:, offset:offset + rows].reshape((count,) + block.shape)
        piece = jnp.moveaxis(piece, 0, axis)
        shape = list(block.shape)
        shape[axis] *= count
        outs.append(piece.reshape(shape))
        offset += rows
    return outs


def flash_body(len_ref, q_ref, kc_ref, vc_ref, kn_ref, vn_ref, o_ref, m_sc, l_sc, acc_sc, *, tk, n_cache, scale):
    j = pl.program_id(1)
    length = len_ref[0]
    tq = q_ref.shape[1]

    @pl.when(j == 0)
    def _():
        m_sc[...] = jnp.full(m_sc.shape, NEG_FILL, jnp.float32)
        l_sc[...] = jnp.zeros(l_sc.shape, jnp.float32)
        acc_sc[...] = jnp.zeros(acc_sc.shape, jnp.float32)

    def update(k, v, mask):
        s = lax.dot_general(q_ref[0], k, (((1,), (1,)), ((), ())), preferred_element_type=jnp.float32) * scale
        if mask is not None:
            s = jnp.where(mask, s, NEG_FILL)
        m_prev = m_sc[...]
        m_new = jnp.maximum(m_prev, jnp.max(s, axis=1, keepdims=True))
        alpha = jnp.exp(m_prev - m_new)
        p = jnp.exp(s - m_new)
        if mask is not None:
            p = jnp.where(mask, p, 0.0)
        l_sc[...] = alpha * l_sc[...] + jnp.sum(p, axis=1, keepdims=True)
        acc_sc[...] = alpha * acc_sc[...] + jnp.dot(p.astype(jnp.bfloat16), v, preferred_element_type=jnp.float32)
        m_sc[...] = m_new

    begin = j * tk

    @pl.when((j < n_cache) & (begin + tk <= length))
    def _():
        update(kc_ref[0], vc_ref[0], None)

    @pl.when((j < n_cache) & (begin < length) & (begin + tk > length))
    def _():
        col = begin + lax.broadcasted_iota(jnp.int32, (tq, tk), 1)
        update(kc_ref[0], vc_ref[0], col < length)

    @pl.when(j == n_cache)
    def _():
        row = lax.broadcasted_iota(jnp.int32, (tq, tq), 0)
        col = lax.broadcasted_iota(jnp.int32, (tq, tq), 1)
        update(kn_ref[0], vn_ref[0], row >= col)
        o_ref[0] = (acc_sc[...] / l_sc[...]).astype(o_ref.dtype)


def flash_attention(length, q, kc, vc, kn, vn):
    heads, new_count, hd = q.shape
    slots = kc.shape[1]
    tk = min(new_count, slots)
    n_cache = slots // tk
    body = functools.partial(flash_body, tk=tk, n_cache=n_cache, scale=hd ** (-0.5))

    def cache_map(h, j, len_ref):
        last = jnp.maximum(len_ref[0] - 1, 0) // tk
        return (h, jnp.minimum(j, last), 0)

    fixed = lambda h, j, len_ref: (h, 0, 0)
    grid_spec = pltpu.PrefetchScalarGridSpec(
        num_scalar_prefetch=1,
        grid=(heads, n_cache + 1),
        in_specs=[
            pl.BlockSpec((1, new_count, hd), fixed),
            pl.BlockSpec((1, tk, hd), cache_map),
            pl.BlockSpec((1, tk, hd), cache_map),
            pl.BlockSpec((1, new_count, hd), fixed),
            pl.BlockSpec((1, new_count, hd), fixed),
        ],
        out_specs=pl.BlockSpec((1, new_count, hd), fixed),
        scratch_shapes=[
            pltpu.VMEM((new_count, 1), jnp.float32),
            pltpu.VMEM((new_count, 1), jnp.float32),
            pltpu.VMEM((new_count, hd), jnp.float32),
        ],
    )
    flops = 4 * heads * new_count * (slots + new_count) * hd
    cost = pl.CostEstimate(
        flops=flops,
        transcendentals=heads * new_count * (slots + new_count),
        bytes_accessed=2 * (q.size + kc.size + vc.size + kn.size + vn.size) + 4 * q.size,
    )
    return pl.pallas_call(
        body,
        grid_spec=grid_spec,
        out_shape=jax.ShapeDtypeStruct((heads, new_count, hd), jnp.bfloat16),
        compiler_params=pltpu.CompilerParams(
            dimension_semantics=("arbitrary", "arbitrary"), vmem_limit_bytes=56 * 1024 * 1024
        ),
        cost_estimate=cost,
    )(length, q, kc, vc, kn, vn)


def on_device(
    hidden_in, w_qkv, w_out, attn_gain, mlp_gain, w_gate, w_up, w_down, k_cache, v_cache, cache_len
):
    new_count = hidden_in.shape[0]
    qkv_shifted, row, col = gather_req_shifted(w_qkv, 1, "req")
    side = qkv_shifted.shape[1]
    w_qkv_full = qkv_shifted.reshape(3, -1, w_qkv.shape[2])
    w_gate_full, w_up_full, w_down_full, w_out_full = gather_packed(
        [w_gate, w_up, w_down, w_out], [0, 0, 1, 1], "req"
    )
    width = w_qkv.shape[2]
    heads_local = width // HD
    slots = k_cache.shape[1]
    full_rows = lax.all_gather(hidden_in, "mp", axis=1, tiled=True)
    normed = rms_scale(full_rows, attn_gain)
    blocks = normed.reshape(new_count, side, side, -1)
    columns = jnp.roll(blocks, (-row, -col), axis=(1, 2)).reshape(new_count, -1)
    projected = jnp.einsum(
        "nd,kdw->knw",
        columns,
        w_qkv_full,
        preferred_element_type=jnp.float32,
    )
    half = HD // 2
    dim = w_qkv_full.shape[1]
    swapped = w_qkv_full[:2].reshape(2, dim, heads_local, 2, half)[:, :, :, ::-1, :]
    partner = jnp.einsum(
        "nd,kdw->knw",
        columns,
        swapped.reshape(2, dim, width),
        preferred_element_type=jnp.float32,
    )
    length = cache_len[0]
    positions = (length + jnp.arange(new_count, dtype=jnp.int32)).astype(jnp.float32)
    lane = jnp.arange(width, dtype=jnp.int32) % HD
    freq = THETA ** (-((lane % half).astype(jnp.float32) * 2.0 / HD))
    angle = positions[:, None] * freq[None, :]
    cosine = jnp.cos(angle)
    sine = jnp.where(lane < half, -1.0, 1.0)[None, :] * jnp.sin(angle)
    queries = (projected[0] * cosine + partner[0] * sine).astype(jnp.bfloat16).reshape(
        new_count, heads_local, HD
    )
    fresh_keys = (projected[1] * cosine + partner[1] * sine).astype(jnp.bfloat16).reshape(
        new_count, heads_local, HD
    )
    fresh_values = projected[2].astype(jnp.bfloat16).reshape(new_count, heads_local, HD)
    head_major = lambda array: array.reshape(array.shape[0], heads_local, HD).transpose(1, 0, 2)
    attn_heads = flash_attention(
        cache_len,
        queries.transpose(1, 0, 2),
        head_major(k_cache[0]),
        head_major(v_cache[0]),
        fresh_keys.transpose(1, 0, 2),
        fresh_values.transpose(1, 0, 2),
    )
    attn = attn_heads.transpose(1, 0, 2).reshape(new_count, width)
    partial_value = jnp.dot(
        attn, w_out_full, preferred_element_type=jnp.float32
    )
    summed = lax.psum(partial_value.astype(jnp.bfloat16), "mp").astype(jnp.float32)
    mid_full = (full_rows.astype(jnp.float32) + summed).astype(jnp.bfloat16)
    own = hidden_in.shape[1]
    mid_local = lax.dynamic_slice_in_dim(mid_full, lax.axis_index("mp") * own, own, axis=1)
    normed2 = rms_scale(mid_full, mlp_gain)
    columns = normed2
    gate = jnp.dot(
        columns,
        w_gate_full,
        preferred_element_type=jnp.float32,
    )
    upper = jnp.dot(
        columns, w_up_full, preferred_element_type=jnp.float32
    )
    units = (jax.nn.silu(gate) * upper).astype(jnp.bfloat16)
    terms = jnp.dot(
        units, w_down_full, preferred_element_type=jnp.float32
    )
    reduced = lax.psum_scatter(
        terms.astype(jnp.bfloat16), "mp", scatter_dimension=1, tiled=True
    ).astype(jnp.float32)
    hidden_out = (mid_local.astype(jnp.float32) + reduced).astype(jnp.bfloat16)
    return (
        hidden_out,
        fresh_keys.reshape(new_count, width),
        fresh_values.reshape(new_count, width),
    )


def solution(mesh):
    return jax.shard_map(
        on_device,
        mesh=mesh,
        in_specs=(
            P("req", "mp"),
            P(None, "req", "mp"),
            P("mp", "req"),
            P(),
            P(),
            P("req", "mp"),
            P("req", "mp"),
            P("mp", "req"),
            P("req", None, "mp"),
            P("req", None, "mp"),
            P("req"),
        ),
        out_specs=(P("req", "mp"), P("req", "mp"), P("req", "mp")),
        check_vma=False,
    )
```

```python
import jax
import jax.numpy as jnp
from jax import lax
from jax.sharding import PartitionSpec as P
from jax.experimental import pallas as pl
from jax.experimental.pallas import tpu as pltpu
import functools

HD = 64


THETA = 130000.0
EPSILON = 1e-05
NEG_FILL = -1e30


def rms_scale(rows, gain):
    values = rows.astype(jnp.float32)
    meansq = jnp.mean(values * values, axis=-1, keepdims=True)
    return (values * lax.rsqrt(meansq + EPSILON) * gain.astype(jnp.float32)).astype(jnp.bfloat16)


def rotate(tensor, positions):
    half = tensor.shape[-1] // 2
    freq = THETA ** (-(jnp.arange(half, dtype=jnp.float32) * 2.0 / tensor.shape[-1]))
    angle = positions[:, None, None] * freq[None, None, :]
    cosine = jnp.cos(angle)
    sine = jnp.sin(angle)
    first = tensor[..., :half]
    second = tensor[..., half:]
    return jnp.concatenate(
        [first * cosine - second * sine, second * cosine + first * sine], axis=-1
    )


def gather_req_shifted(block, axis, axis_name):
    count = lax.axis_size(axis_name)
    side = int(round(count ** 0.5))
    me = lax.axis_index(axis_name)
    row, col = me // side, me % side

    def inner(k):
        return [(s, (s // side) * side + (s % side - k) % side) for s in range(count)]

    def outer(k):
        return [(s, ((s // side - k) % side) * side + s % side) for s in range(count)]

    parts = [block] + [lax.ppermute(block, axis_name, inner(k)) for k in range(1, side)]
    stage = jnp.stack(parts, axis=axis)
    parts = [stage] + [lax.ppermute(stage, axis_name, outer(k)) for k in range(1, side)]
    return jnp.stack(parts, axis=axis), row, col


def gather_packed(blocks, axes, axis_name):
    count = lax.axis_size(axis_name)
    lane = 128
    joined = jnp.concatenate([block.reshape(-1, lane) for block in blocks], axis=0)
    gathered = lax.all_gather(joined, axis_name, axis=0, tiled=False)
    outs = []
    offset = 0
    for block, axis in zip(blocks, axes):
        rows = block.size // lane
        piece = gathered[:, offset:offset + rows].reshape((count,) + block.shape)
        piece = jnp.moveaxis(piece, 0, axis)
        shape = list(block.shape)
        shape[axis] *= count
        outs.append(piece.reshape(shape))
        offset += rows
    return outs


def flash_body(len_ref, q_ref, kc_ref, vc_ref, kn_ref, vn_ref, o_ref, m_sc, l_sc, acc_sc, *, tk, n_cache, scale):
    j = pl.program_id(1)
    length = len_ref[0]
    tq = q_ref.shape[1]

    @pl.when(j == 0)
    def _():
        m_sc[...] = jnp.full(m_sc.shape, NEG_FILL, jnp.float32)
        l_sc[...] = jnp.zeros(l_sc.shape, jnp.float32)
        acc_sc[...] = jnp.zeros(acc_sc.shape, jnp.float32)

    def update(k, v, limit_of, chunk):
        def one_chunk(index, carry):
            rows = pl.ds(pl.multiple_of(index * chunk, chunk), chunk)
            s = lax.dot_general(
                q_ref[0, rows], k, (((1,), (1,)), ((), ())), preferred_element_type=jnp.float32
            ) * scale
            row = index * chunk + lax.broadcasted_iota(jnp.int32, s.shape, 0)
            col = lax.broadcasted_iota(jnp.int32, s.shape, 1)
            mask = col < limit_of(row)
            s = jnp.where(mask, s, NEG_FILL)
            m_prev = m_sc[rows]
            m_new = jnp.maximum(m_prev, jnp.max(s, axis=1, keepdims=True))
            alpha = jnp.exp(m_prev - m_new)
            p = jnp.where(mask, jnp.exp(s - m_new), 0.0)
            l_sc[rows] = alpha * l_sc[rows] + jnp.sum(p, axis=1, keepdims=True)
            acc_sc[rows] = alpha * acc_sc[rows] + jnp.dot(
                p.astype(jnp.bfloat16), v, preferred_element_type=jnp.float32
            )
            m_sc[rows] = m_new
            return carry

        lax.fori_loop(0, tq // chunk, one_chunk, 0)

    begin = j * tk
    in_cache = j < n_cache

    @pl.when(jnp.logical_not(in_cache) | (begin < length))
    def _():
        keys = jnp.where(in_cache, kc_ref[0], kn_ref[0])
        values = jnp.where(in_cache, vc_ref[0], vn_ref[0])
        update(keys, values, lambda row: jnp.where(in_cache, length - begin, row + 1), min(tq, 256))

    @pl.when(j == n_cache)
    def _():
        o_ref[0] = (acc_sc[...] / l_sc[...]).astype(o_ref.dtype)


def flash_attention(length, q, kc, vc, kn, vn):
    heads, new_count, hd = q.shape
    slots = kc.shape[1]
    tk = min(new_count, slots)
    n_cache = slots // tk
    body = functools.partial(flash_body, tk=tk, n_cache=n_cache, scale=hd ** (-0.5))

    def cache_map(h, j, len_ref):
        last = jnp.maximum(len_ref[0] - 1, 0) // tk
        return (h, jnp.minimum(j, last), 0)

    fixed = lambda h, j, len_ref: (h, 0, 0)
    grid_spec = pltpu.PrefetchScalarGridSpec(
        num_scalar_prefetch=1,
        grid=(heads, n_cache + 1),
        in_specs=[
            pl.BlockSpec((1, new_count, hd), fixed),
            pl.BlockSpec((1, tk, hd), cache_map),
            pl.BlockSpec((1, tk, hd), cache_map),
            pl.BlockSpec((1, new_count, hd), fixed),
            pl.BlockSpec((1, new_count, hd), fixed),
        ],
        out_specs=pl.BlockSpec((1, new_count, hd), fixed),
        scratch_shapes=[
            pltpu.VMEM((new_count, 1), jnp.float32),
            pltpu.VMEM((new_count, 1), jnp.float32),
            pltpu.VMEM((new_count, hd), jnp.float32),
        ],
    )
    flops = 4 * heads * new_count * (slots + new_count) * hd
    cost = pl.CostEstimate(
        flops=flops,
        transcendentals=heads * new_count * (slots + new_count),
        bytes_accessed=2 * (q.size + kc.size + vc.size + kn.size + vn.size) + 4 * q.size,
    )
    return pl.pallas_call(
        body,
        grid_spec=grid_spec,
        out_shape=jax.ShapeDtypeStruct((heads, new_count, hd), jnp.bfloat16),
        compiler_params=pltpu.CompilerParams(
            dimension_semantics=("arbitrary", "arbitrary"), vmem_limit_bytes=56 * 1024 * 1024
        ),
        cost_estimate=cost,
    )(length, q, kc, vc, kn, vn)


def on_device(
    hidden_in, w_qkv, w_out, attn_gain, mlp_gain, w_gate, w_up, w_down, k_cache, v_cache, cache_len
):
    new_count = hidden_in.shape[0]
    qkv_shifted, row, col = gather_req_shifted(w_qkv, 1, "req")
    side = qkv_shifted.shape[1]
    w_qkv_full = qkv_shifted.reshape(3, -1, w_qkv.shape[2])
    w_gate_full, w_up_full, w_down_full, w_out_full = gather_packed(
        [w_gate, w_up, w_down, w_out], [0, 0, 1, 1], "req"
    )
    width = w_qkv.shape[2]
    heads_local = width // HD
    slots = k_cache.shape[1]
    full_rows = lax.all_gather(hidden_in, "mp", axis=1, tiled=True)
    normed = rms_scale(full_rows, attn_gain)
    blocks = normed.reshape(new_count, side, side, -1)
    columns = jnp.roll(blocks, (-row, -col), axis=(1, 2)).reshape(new_count, -1)
    projected = jnp.einsum(
        "nd,kdw->knw",
        columns,
        w_qkv_full,
        preferred_element_type=jnp.float32,
    )
    length = cache_len[0]
    positions = (length + jnp.arange(new_count, dtype=jnp.int32)).astype(jnp.float32)
    queries = rotate(projected[0].reshape(new_count, heads_local, HD), positions).astype(
        jnp.bfloat16
    )
    fresh_keys = rotate(projected[1].reshape(new_count, heads_local, HD), positions).astype(
        jnp.bfloat16
    )
    fresh_values = projected[2].astype(jnp.bfloat16).reshape(new_count, heads_local, HD)
    head_major = lambda array: array.reshape(array.shape[0], heads_local, HD).transpose(1, 0, 2)
    attn_heads = flash_attention(
        cache_len,
        queries.transpose(1, 0, 2),
        head_major(k_cache[0]),
        head_major(v_cache[0]),
        fresh_keys.transpose(1, 0, 2),
        fresh_values.transpose(1, 0, 2),
    )
    attn = attn_heads.transpose(1, 0, 2).reshape(new_count, width)
    partial_value = jnp.dot(
        attn, w_out_full, preferred_element_type=jnp.float32
    )
    summed = lax.psum(partial_value.astype(jnp.bfloat16), "mp").astype(jnp.float32)
    mid_full = (full_rows.astype(jnp.float32) + summed).astype(jnp.bfloat16)
    own = hidden_in.shape[1]
    mid_local = lax.dynamic_slice_in_dim(mid_full, lax.axis_index("mp") * own, own, axis=1)
    normed2 = rms_scale(mid_full, mlp_gain)
    columns = normed2
    gate = jnp.dot(
        columns,
        w_gate_full,
        preferred_element_type=jnp.float32,
    )
    upper = jnp.dot(
        columns, w_up_full, preferred_element_type=jnp.float32
    )
    units = (jax.nn.silu(gate) * upper).astype(jnp.bfloat16)
    terms = jnp.dot(
        units, w_down_full, preferred_element_type=jnp.float32
    )
    reduced = lax.psum_scatter(
        terms.astype(jnp.bfloat16), "mp", scatter_dimension=1, tiled=True
    ).astype(jnp.float32)
    hidden_out = (mid_local.astype(jnp.float32) + reduced).astype(jnp.bfloat16)
    return (
        hidden_out,
        fresh_keys.reshape(new_count, width),
        fresh_values.reshape(new_count, width),
    )


def solution(mesh):
    return jax.shard_map(
        on_device,
        mesh=mesh,
        in_specs=(
            P("req", "mp"),
            P(None, "req", "mp"),
            P("mp", "req"),
            P(),
            P(),
            P("req", "mp"),
            P("req", "mp"),
            P("mp", "req"),
            P("req", None, "mp"),
            P("req", None, "mp"),
            P("req"),
        ),
        out_specs=(P("req", "mp"), P("req", "mp"), P("req", "mp")),
        check_vma=False,
    )
```

```python
import jax
import jax.numpy as jnp
from jax import lax
from jax.sharding import PartitionSpec as P
from jax.experimental import pallas as pl
from jax.experimental.pallas import tpu as pltpu
import functools

HD = 64


THETA = 130000.0
EPSILON = 1e-05
NEG_FILL = -1e30


def rms_scale(rows, gain):
    values = rows.astype(jnp.float32)
    meansq = jnp.mean(values * values, axis=-1, keepdims=True)
    return (values * lax.rsqrt(meansq + EPSILON) * gain.astype(jnp.float32)).astype(jnp.bfloat16)


def gather_req_shifted(block, axis, axis_name):
    count = lax.axis_size(axis_name)
    side = int(round(count ** 0.5))
    me = lax.axis_index(axis_name)
    row, col = me // side, me % side

    def inner(k):
        return [(s, (s // side) * side + (s % side - k) % side) for s in range(count)]

    def outer(k):
        return [(s, ((s // side - k) % side) * side + s % side) for s in range(count)]

    parts = [block] + [lax.ppermute(block, axis_name, inner(k)) for k in range(1, side)]
    stage = jnp.stack(parts, axis=axis)
    parts = [stage] + [lax.ppermute(stage, axis_name, outer(k)) for k in range(1, side)]
    return jnp.stack(parts, axis=axis), row, col


def gather_packed(blocks, axes, axis_name):
    count = lax.axis_size(axis_name)
    lane = 128
    joined = jnp.concatenate([block.reshape(-1, lane) for block in blocks], axis=0)
    gathered = lax.all_gather(joined, axis_name, axis=0, tiled=False)
    outs = []
    offset = 0
    for block, axis in zip(blocks, axes):
        rows = block.size // lane
        piece = gathered[:, offset:offset + rows].reshape((count,) + block.shape)
        piece = jnp.moveaxis(piece, 0, axis)
        shape = list(block.shape)
        shape[axis] *= count
        outs.append(piece.reshape(shape))
        offset += rows
    return outs


def flash_body(len_ref, q_ref, kc_ref, vc_ref, kn_ref, vn_ref, o_ref, m_sc, l_sc, acc_sc, *, tk, n_cache, scale):
    j = pl.program_id(1)
    length = len_ref[0]
    tq = q_ref.shape[1]

    @pl.when(j == 0)
    def _():
        m_sc[...] = jnp.full(m_sc.shape, NEG_FILL, jnp.float32)
        l_sc[...] = jnp.zeros(l_sc.shape, jnp.float32)
        acc_sc[...] = jnp.zeros(acc_sc.shape, jnp.float32)

    def update(k, v, mask):
        s = lax.dot_general(q_ref[0] * scale, k, (((1,), (1,)), ((), ())), preferred_element_type=jnp.float32)
        if mask is not None:
            s = jnp.where(mask, s, NEG_FILL)
        m_prev = m_sc[...]
        m_new = jnp.maximum(m_prev, jnp.max(s, axis=1, keepdims=True))
        alpha = jnp.exp(m_prev - m_new)
        p = jnp.exp(s - m_new)
        if mask is not None:
            p = jnp.where(mask, p, 0.0)
        l_sc[...] = alpha * l_sc[...] + jnp.sum(p, axis=1, keepdims=True)
        acc_sc[...] = alpha * acc_sc[...] + jnp.dot(p.astype(jnp.bfloat16), v, preferred_element_type=jnp.float32)
        m_sc[...] = m_new

    begin = j * tk

    @pl.when((j < n_cache) & (begin + tk <= length))
    def _():
        update(kc_ref[0], vc_ref[0], None)

    @pl.when((j < n_cache) & (begin < length) & (begin + tk > length))
    def _():
        col = begin + lax.broadcasted_iota(jnp.int32, (tq, tk), 1)
        update(kc_ref[0], vc_ref[0], col < length)

    @pl.when(j == n_cache)
    def _():
        row = lax.broadcasted_iota(jnp.int32, (tq, tq), 0)
        col = lax.broadcasted_iota(jnp.int32, (tq, tq), 1)
        update(kn_ref[0], vn_ref[0], row >= col)
        o_ref[0] = (acc_sc[...] / l_sc[...]).astype(o_ref.dtype)


def flash_attention(length, q, kc, vc, kn, vn):
    heads, new_count, hd = q.shape
    slots = kc.shape[1]
    tk = min(new_count, slots)
    n_cache = slots // tk
    body = functools.partial(flash_body, tk=tk, n_cache=n_cache, scale=hd ** (-0.5))

    def cache_map(h, j, len_ref):
        last = jnp.maximum(len_ref[0] - 1, 0) // tk
        return (h, jnp.minimum(j, last), 0)

    fixed = lambda h, j, len_ref: (h, 0, 0)
    grid_spec = pltpu.PrefetchScalarGridSpec(
        num_scalar_prefetch=1,
        grid=(heads, n_cache + 1),
        in_specs=[
            pl.BlockSpec((1, new_count, hd), fixed),
            pl.BlockSpec((1, tk, hd), cache_map),
            pl.BlockSpec((1, tk, hd), cache_map),
            pl.BlockSpec((1, new_count, hd), fixed),
            pl.BlockSpec((1, new_count, hd), fixed),
        ],
        out_specs=pl.BlockSpec((1, new_count, hd), fixed),
        scratch_shapes=[
            pltpu.VMEM((new_count, 1), jnp.float32),
            pltpu.VMEM((new_count, 1), jnp.float32),
            pltpu.VMEM((new_count, hd), jnp.float32),
        ],
    )
    flops = 4 * heads * new_count * (slots + new_count) * hd
    cost = pl.CostEstimate(
        flops=flops,
        transcendentals=heads * new_count * (slots + new_count),
        bytes_accessed=2 * (q.size + kc.size + vc.size + kn.size + vn.size) + 4 * q.size,
    )
    return pl.pallas_call(
        body,
        grid_spec=grid_spec,
        out_shape=jax.ShapeDtypeStruct((heads, new_count, hd), jnp.bfloat16),
        compiler_params=pltpu.CompilerParams(
            dimension_semantics=("arbitrary", "arbitrary"), vmem_limit_bytes=56 * 1024 * 1024
        ),
        cost_estimate=cost,
    )(length, q, kc, vc, kn, vn)


def on_device(
    hidden_in, w_qkv, w_out, attn_gain, mlp_gain, w_gate, w_up, w_down, k_cache, v_cache, cache_len
):
    new_count = hidden_in.shape[0]
    qkv_shifted, row, col = gather_req_shifted(w_qkv, 1, "req")
    side = qkv_shifted.shape[1]
    w_qkv_full = qkv_shifted.reshape(3, -1, w_qkv.shape[2])
    w_gate_full, w_up_full, w_down_full, w_out_full = gather_packed(
        [w_gate, w_up, w_down, w_out], [0, 0, 1, 1], "req"
    )
    width = w_qkv.shape[2]
    heads_local = width // HD
    slots = k_cache.shape[1]
    full_rows = lax.all_gather(hidden_in, "mp", axis=1, tiled=True)
    normed = rms_scale(full_rows, attn_gain)
    blocks = normed.reshape(new_count, side, side, -1)
    columns = jnp.roll(blocks, (-row, -col), axis=(1, 2)).reshape(new_count, -1)
    projected = jnp.einsum(
        "nd,kdw->knw",
        columns,
        w_qkv_full,
        preferred_element_type=jnp.float32,
    )
    length = cache_len[0]
    positions = (length + jnp.arange(new_count, dtype=jnp.int32)).astype(jnp.float32)
    half = HD // 2
    lane = jnp.arange(width, dtype=jnp.int32)
    within = lane % HD
    partner_lane = lane - within + (within + half) % HD
    swap = (lane[:, None] == partner_lane[None, :]).astype(jnp.float32)
    partner = jnp.einsum(
        "knw,wv->knv", projected[:2], swap, precision=lax.Precision.HIGHEST,
        preferred_element_type=jnp.float32,
    )
    freq = THETA ** (-((within % half).astype(jnp.float32) * 2.0 / HD))
    angle = positions[:, None] * freq[None, :]
    cosine = jnp.cos(angle)
    sine = jnp.where(within < half, -1.0, 1.0)[None, :] * jnp.sin(angle)
    queries = (projected[0] * cosine + partner[0] * sine).astype(jnp.bfloat16).reshape(
        new_count, heads_local, HD
    )
    fresh_keys = (projected[1] * cosine + partner[1] * sine).astype(jnp.bfloat16).reshape(
        new_count, heads_local, HD
    )
    fresh_values = projected[2].astype(jnp.bfloat16).reshape(new_count, heads_local, HD)
    head_major = lambda array: array.reshape(array.shape[0], heads_local, HD).transpose(1, 0, 2)
    attn_heads = flash_attention(
        cache_len,
        queries.transpose(1, 0, 2),
        head_major(k_cache[0]),
        head_major(v_cache[0]),
        fresh_keys.transpose(1, 0, 2),
        fresh_values.transpose(1, 0, 2),
    )
    attn = attn_heads.transpose(1, 0, 2).reshape(new_count, width)
    partial_value = jnp.dot(
        attn, w_out_full, preferred_element_type=jnp.float32
    )
    summed = lax.psum(partial_value.astype(jnp.bfloat16), "mp").astype(jnp.float32)
    mid_full = (full_rows.astype(jnp.float32) + summed).astype(jnp.bfloat16)
    own = hidden_in.shape[1]
    mid_local = lax.dynamic_slice_in_dim(mid_full, lax.axis_index("mp") * own, own, axis=1)
    normed2 = rms_scale(mid_full, mlp_gain)
    columns = normed2
    gate = jnp.dot(
        columns,
        w_gate_full,
        preferred_element_type=jnp.float32,
    )
    upper = jnp.dot(
        columns, w_up_full, preferred_element_type=jnp.float32
    )
    units = (jax.nn.silu(gate) * upper).astype(jnp.bfloat16)
    terms = jnp.dot(
        units, w_down_full, preferred_element_type=jnp.float32
    )
    reduced = lax.psum_scatter(
        terms.astype(jnp.bfloat16), "mp", scatter_dimension=1, tiled=True
    ).astype(jnp.float32)
    hidden_out = (mid_local.astype(jnp.float32) + reduced).astype(jnp.bfloat16)
    return (
        hidden_out,
        fresh_keys.reshape(new_count, width),
        fresh_values.reshape(new_count, width),
    )


def solution(mesh):
    return jax.shard_map(
        on_device,
        mesh=mesh,
        in_specs=(
            P("req", "mp"),
            P(None, "req", "mp"),
            P("mp", "req"),
            P(),
            P(),
            P("req", "mp"),
            P("req", "mp"),
            P("mp", "req"),
            P("req", None, "mp"),
            P("req", None, "mp"),
            P("req"),
        ),
        out_specs=(P("req", "mp"), P("req", "mp"), P("req", "mp")),
        check_vma=False,
    )
```

```python
import jax
import jax.numpy as jnp
from jax import lax
from jax.sharding import PartitionSpec as P
from jax.experimental import pallas as pl
from jax.experimental.pallas import tpu as pltpu
import functools

HD = 64


THETA = 130000.0
EPSILON = 1e-05
NEG_FILL = -1e30


def rms_scale(rows, gain):
    values = rows.astype(jnp.float32)
    meansq = jnp.mean(values * values, axis=-1, keepdims=True)
    return (values * lax.rsqrt(meansq + EPSILON) * gain.astype(jnp.float32)).astype(jnp.bfloat16)


def gather_req_shifted(block, axis, axis_name):
    count = lax.axis_size(axis_name)
    side = int(round(count ** 0.5))
    me = lax.axis_index(axis_name)
    row, col = me // side, me % side

    def inner(k):
        return [(s, (s // side) * side + (s % side - k) % side) for s in range(count)]

    def outer(k):
        return [(s, ((s // side - k) % side) * side + s % side) for s in range(count)]

    parts = [block] + [lax.ppermute(block, axis_name, inner(k)) for k in range(1, side)]
    stage = jnp.stack(parts, axis=axis)
    parts = [stage] + [lax.ppermute(stage, axis_name, outer(k)) for k in range(1, side)]
    return jnp.stack(parts, axis=axis), row, col


def gather_packed(blocks, axes, axis_name):
    count = lax.axis_size(axis_name)
    lane = 128
    joined = jnp.concatenate([block.reshape(-1, lane) for block in blocks], axis=0)
    gathered = lax.all_gather(joined, axis_name, axis=0, tiled=False)
    outs = []
    offset = 0
    for block, axis in zip(blocks, axes):
        rows = block.size // lane
        piece = gathered[:, offset:offset + rows].reshape((count,) + block.shape)
        piece = jnp.moveaxis(piece, 0, axis)
        shape = list(block.shape)
        shape[axis] *= count
        outs.append(piece.reshape(shape))
        offset += rows
    return outs


def flash_body(len_ref, q_ref, kc_ref, vc_ref, kn_ref, vn_ref, o_ref, m_sc, l_sc, acc_sc, *, tk, n_cache, scale):
    j = pl.program_id(1)
    length = len_ref[0]
    tq = q_ref.shape[0]
    pair = q_ref.shape[1] // HD

    @pl.when(j == 0)
    def _():
        m_sc[...] = jnp.full(m_sc.shape, NEG_FILL, jnp.float32)
        l_sc[...] = jnp.zeros(l_sc.shape, jnp.float32)
        acc_sc[...] = jnp.zeros(acc_sc.shape, jnp.float32)

    def update(k_ref, v_ref, mask):
        for head in range(pair):
            lanes = pl.ds(head * HD, HD)
            q = q_ref[:, lanes] * scale
            s = lax.dot_general(q, k_ref[:, lanes], (((1,), (1,)), ((), ())), preferred_element_type=jnp.float32)
            if mask is not None:
                s = jnp.where(mask, s, NEG_FILL)
            m_prev = m_sc[head]
            m_new = jnp.maximum(m_prev, jnp.max(s, axis=1, keepdims=True))
            alpha = jnp.exp(m_prev - m_new)
            p = jnp.exp(s - m_new)
            if mask is not None:
                p = jnp.where(mask, p, 0.0)
            l_sc[head] = alpha * l_sc[head] + jnp.sum(p, axis=1, keepdims=True)
            acc_sc[head] = alpha * acc_sc[head] + jnp.dot(
                p.astype(jnp.bfloat16), v_ref[:, lanes], preferred_element_type=jnp.float32
            )
            m_sc[head] = m_new

    begin = j * tk

    @pl.when((j < n_cache) & (begin + tk <= length))
    def _():
        update(kc_ref, vc_ref, None)

    @pl.when((j < n_cache) & (begin < length) & (begin + tk > length))
    def _():
        col = begin + lax.broadcasted_iota(jnp.int32, (tq, tk), 1)
        update(kc_ref, vc_ref, col < length)

    @pl.when(j == n_cache)
    def _():
        row = lax.broadcasted_iota(jnp.int32, (tq, tq), 0)
        col = lax.broadcasted_iota(jnp.int32, (tq, tq), 1)
        update(kn_ref, vn_ref, row >= col)
        for head in range(pair):
            o_ref[:, pl.ds(head * HD, HD)] = (acc_sc[head] / l_sc[head]).astype(o_ref.dtype)


def flash_attention(length, q, kc, vc, kn, vn):
    new_count, width = q.shape
    slots = kc.shape[0]
    tk = min(new_count, slots)
    n_cache = slots // tk
    lanes = 2 * HD if width % (2 * HD) == 0 else width
    pair = lanes // HD
    body = functools.partial(flash_body, tk=tk, n_cache=n_cache, scale=HD ** (-0.5))

    def cache_map(h, j, len_ref):
        last = jnp.maximum(len_ref[0] - 1, 0) // tk
        return (jnp.minimum(j, last), h)

    fixed = lambda h, j, len_ref: (0, h)
    grid_spec = pltpu.PrefetchScalarGridSpec(
        num_scalar_prefetch=1,
        grid=(width // lanes, n_cache + 1),
        in_specs=[
            pl.BlockSpec((new_count, lanes), fixed),
            pl.BlockSpec((tk, lanes), cache_map),
            pl.BlockSpec((tk, lanes), cache_map),
            pl.BlockSpec((new_count, lanes), fixed),
            pl.BlockSpec((new_count, lanes), fixed),
        ],
        out_specs=pl.BlockSpec((new_count, lanes), fixed),
        scratch_shapes=[
            pltpu.VMEM((pair, new_count, 1), jnp.float32),
            pltpu.VMEM((pair, new_count, 1), jnp.float32),
            pltpu.VMEM((pair, new_count, HD), jnp.float32),
        ],
    )
    heads = width // HD
    cost = pl.CostEstimate(
        flops=4 * heads * new_count * (slots + new_count) * HD,
        transcendentals=heads * new_count * (slots + new_count),
        bytes_accessed=2 * (q.size + kc.size + vc.size + kn.size + vn.size) + 2 * q.size,
    )
    return pl.pallas_call(
        body,
        grid_spec=grid_spec,
        out_shape=jax.ShapeDtypeStruct((new_count, width), jnp.bfloat16),
        compiler_params=pltpu.CompilerParams(
            dimension_semantics=("arbitrary", "arbitrary"), vmem_limit_bytes=56 * 1024 * 1024
        ),
        cost_estimate=cost,
    )(length, q, kc, vc, kn, vn)


def on_device(
    hidden_in, w_qkv, w_out, attn_gain, mlp_gain, w_gate, w_up, w_down, k_cache, v_cache, cache_len
):
    new_count = hidden_in.shape[0]
    qkv_shifted, row, col = gather_req_shifted(w_qkv, 1, "req")
    side = qkv_shifted.shape[1]
    w_qkv_full = qkv_shifted.reshape(3, -1, w_qkv.shape[2])
    w_gate_full, w_up_full, w_down_full, w_out_full = gather_packed(
        [w_gate, w_up, w_down, w_out], [0, 0, 1, 1], "req"
    )
    width = w_qkv.shape[2]
    heads_local = width // HD
    slots = k_cache.shape[1]
    full_rows = lax.all_gather(hidden_in, "mp", axis=1, tiled=True)
    normed = rms_scale(full_rows, attn_gain)
    blocks = normed.reshape(new_count, side, side, -1)
    columns = jnp.roll(blocks, (-row, -col), axis=(1, 2)).reshape(new_count, -1)
    projected = jnp.einsum(
        "nd,kdw->knw",
        columns,
        w_qkv_full,
        preferred_element_type=jnp.float32,
    )
    length = cache_len[0]
    positions = (length + jnp.arange(new_count, dtype=jnp.int32)).astype(jnp.float32)
    half = HD // 2
    lane = jnp.arange(width, dtype=jnp.int32)
    within = lane % HD
    partner_lane = lane - within + (within + half) % HD
    swap = (lane[:, None] == partner_lane[None, :]).astype(jnp.float32)
    partner = jnp.einsum(
        "knw,wv->knv", projected[:2], swap, precision=lax.Precision.HIGHEST,
        preferred_element_type=jnp.float32,
    )
    freq = THETA ** (-((within % half).astype(jnp.float32) * 2.0 / HD))
    angle = positions[:, None] * freq[None, :]
    cosine = jnp.cos(angle)
    sine = jnp.where(within < half, -1.0, 1.0)[None, :] * jnp.sin(angle)
    queries = (projected[0] * cosine + partner[0] * sine).astype(jnp.bfloat16).reshape(
        new_count, heads_local, HD
    )
    fresh_keys = (projected[1] * cosine + partner[1] * sine).astype(jnp.bfloat16).reshape(
        new_count, heads_local, HD
    )
    fresh_values = projected[2].astype(jnp.bfloat16).reshape(new_count, heads_local, HD)
    attn = flash_attention(
        cache_len,
        queries.reshape(new_count, width),
        k_cache[0],
        v_cache[0],
        fresh_keys.reshape(new_count, width),
        fresh_values.reshape(new_count, width),
    )
    partial_value = jnp.dot(
        attn, w_out_full, preferred_element_type=jnp.float32
    )
    summed = lax.psum(partial_value.astype(jnp.bfloat16), "mp").astype(jnp.float32)
    mid_full = (full_rows.astype(jnp.float32) + summed).astype(jnp.bfloat16)
    own = hidden_in.shape[1]
    mid_local = lax.dynamic_slice_in_dim(mid_full, lax.axis_index("mp") * own, own, axis=1)
    normed2 = rms_scale(mid_full, mlp_gain)
    columns = normed2
    gate = jnp.dot(
        columns,
        w_gate_full,
        preferred_element_type=jnp.float32,
    )
    upper = jnp.dot(
        columns, w_up_full, preferred_element_type=jnp.float32
    )
    units = (jax.nn.silu(gate) * upper).astype(jnp.bfloat16)
    terms = jnp.dot(
        units, w_down_full, preferred_element_type=jnp.float32
    )
    reduced = lax.psum_scatter(
        terms.astype(jnp.bfloat16), "mp", scatter_dimension=1, tiled=True
    ).astype(jnp.float32)
    hidden_out = (mid_local.astype(jnp.float32) + reduced).astype(jnp.bfloat16)
    return (
        hidden_out,
        fresh_keys.reshape(new_count, width),
        fresh_values.reshape(new_count, width),
    )


def solution(mesh):
    return jax.shard_map(
        on_device,
        mesh=mesh,
        in_specs=(
            P("req", "mp"),
            P(None, "req", "mp"),
            P("mp", "req"),
            P(),
            P(),
            P("req", "mp"),
            P("req", "mp"),
            P("mp", "req"),
            P("req", None, "mp"),
            P("req", None, "mp"),
            P("req"),
        ),
        out_specs=(P("req", "mp"), P("req", "mp"), P("req", "mp")),
        check_vma=False,
    )
```

```python
import jax
import jax.numpy as jnp
from jax import lax
from jax.sharding import PartitionSpec as P
from jax.experimental import pallas as pl
from jax.experimental.pallas import tpu as pltpu
import functools

HD = 64


THETA = 130000.0
EPSILON = 1e-05
NEG_FILL = -1e30


def rms_scale(rows, gain):
    values = rows.astype(jnp.float32)
    meansq = jnp.mean(values * values, axis=-1, keepdims=True)
    return (values * lax.rsqrt(meansq + EPSILON) * gain.astype(jnp.float32)).astype(jnp.bfloat16)


def gather_req_shifted(block, axis, axis_name):
    count = lax.axis_size(axis_name)
    side = int(round(count ** 0.5))
    me = lax.axis_index(axis_name)
    row, col = me // side, me % side

    def inner(k):
        return [(s, (s // side) * side + (s % side - k) % side) for s in range(count)]

    def outer(k):
        return [(s, ((s // side - k) % side) * side + s % side) for s in range(count)]

    parts = [block] + [lax.ppermute(block, axis_name, inner(k)) for k in range(1, side)]
    stage = jnp.stack(parts, axis=axis)
    parts = [stage] + [lax.ppermute(stage, axis_name, outer(k)) for k in range(1, side)]
    return jnp.stack(parts, axis=axis), row, col


def gather_packed(blocks, axes, axis_name):
    count = lax.axis_size(axis_name)
    lane = 128
    joined = jnp.concatenate([block.reshape(-1, lane) for block in blocks], axis=0)
    gathered = lax.all_gather(joined, axis_name, axis=0, tiled=False)
    outs = []
    offset = 0
    for block, axis in zip(blocks, axes):
        rows = block.size // lane
        piece = gathered[:, offset:offset + rows].reshape((count,) + block.shape)
        piece = jnp.moveaxis(piece, 0, axis)
        shape = list(block.shape)
        shape[axis] *= count
        outs.append(piece.reshape(shape))
        offset += rows
    return outs


def flash_body(len_ref, q_ref, kc_ref, vc_ref, kn_ref, vn_ref, o_ref, m_sc, l_sc, acc_sc, *, tk, n_cache, scale):
    j = pl.program_id(1)
    length = len_ref[0]
    tq = q_ref.shape[0]
    pair = q_ref.shape[1] // HD

    @pl.when(j == 0)
    def _():
        m_sc[...] = jnp.full(m_sc.shape, NEG_FILL, jnp.float32)
        l_sc[...] = jnp.zeros(l_sc.shape, jnp.float32)
        acc_sc[...] = jnp.zeros(acc_sc.shape, jnp.float32)

    def update(keys_of, values_of, mask):
        for head in range(pair):
            lanes = pl.ds(head * HD, HD)
            q = q_ref[:, lanes] * scale
            s = lax.dot_general(q, keys_of(lanes), (((1,), (1,)), ((), ())), preferred_element_type=jnp.float32)
            if mask is not None:
                s = jnp.where(mask, s, NEG_FILL)
            m_prev = m_sc[head]
            m_new = jnp.maximum(m_prev, jnp.max(s, axis=1, keepdims=True))
            alpha = jnp.exp(m_prev - m_new)
            p = jnp.exp(s - m_new)
            if mask is not None:
                p = jnp.where(mask, p, 0.0)
            l_sc[head] = alpha * l_sc[head] + jnp.sum(p, axis=1, keepdims=True)
            acc_sc[head] = alpha * acc_sc[head] + jnp.dot(
                p.astype(jnp.bfloat16), values_of(lanes), preferred_element_type=jnp.float32
            )
            m_sc[head] = m_new

    begin = j * tk
    in_cache = j < n_cache

    @pl.when(jnp.logical_not(in_cache) | (begin < length))
    def _():
        row = lax.broadcasted_iota(jnp.int32, (tq, tk), 0)
        col = lax.broadcasted_iota(jnp.int32, (tq, tk), 1)
        mask = col < jnp.where(in_cache, length - begin, row + 1)
        update(
            lambda lanes: jnp.where(in_cache, kc_ref[:, lanes], kn_ref[:, lanes]),
            lambda lanes: jnp.where(in_cache, vc_ref[:, lanes], vn_ref[:, lanes]),
            mask,
        )

    @pl.when(j == n_cache)
    def _():
        for head in range(pair):
            o_ref[:, pl.ds(head * HD, HD)] = (acc_sc[head] / l_sc[head]).astype(o_ref.dtype)


def flash_attention(length, q, kc, vc, kn, vn):
    new_count, width = q.shape
    slots = kc.shape[0]
    tk = min(new_count, slots)
    n_cache = slots // tk
    lanes = 2 * HD if width % (2 * HD) == 0 else width
    pair = lanes // HD
    body = functools.partial(flash_body, tk=tk, n_cache=n_cache, scale=HD ** (-0.5))

    def cache_map(h, j, len_ref):
        last = jnp.maximum(len_ref[0] - 1, 0) // tk
        return (jnp.minimum(j, last), h)

    fixed = lambda h, j, len_ref: (0, h)
    grid_spec = pltpu.PrefetchScalarGridSpec(
        num_scalar_prefetch=1,
        grid=(width // lanes, n_cache + 1),
        in_specs=[
            pl.BlockSpec((new_count, lanes), fixed),
            pl.BlockSpec((tk, lanes), cache_map),
            pl.BlockSpec((tk, lanes), cache_map),
            pl.BlockSpec((new_count, lanes), fixed),
            pl.BlockSpec((new_count, lanes), fixed),
        ],
        out_specs=pl.BlockSpec((new_count, lanes), fixed),
        scratch_shapes=[
            pltpu.VMEM((pair, new_count, 1), jnp.float32),
            pltpu.VMEM((pair, new_count, 1), jnp.float32),
            pltpu.VMEM((pair, new_count, HD), jnp.float32),
        ],
    )
    heads = width // HD
    cost = pl.CostEstimate(
        flops=4 * heads * new_count * (slots + new_count) * HD,
        transcendentals=heads * new_count * (slots + new_count),
        bytes_accessed=2 * (q.size + kc.size + vc.size + kn.size + vn.size) + 2 * q.size,
    )
    return pl.pallas_call(
        body,
        grid_spec=grid_spec,
        out_shape=jax.ShapeDtypeStruct((new_count, width), jnp.bfloat16),
        compiler_params=pltpu.CompilerParams(
            dimension_semantics=("arbitrary", "arbitrary"), vmem_limit_bytes=56 * 1024 * 1024
        ),
        cost_estimate=cost,
    )(length, q, kc, vc, kn, vn)


def on_device(
    hidden_in, w_qkv, w_out, attn_gain, mlp_gain, w_gate, w_up, w_down, k_cache, v_cache, cache_len
):
    new_count = hidden_in.shape[0]
    qkv_shifted, row, col = gather_req_shifted(w_qkv, 1, "req")
    side = qkv_shifted.shape[1]
    w_qkv_full = qkv_shifted.reshape(3, -1, w_qkv.shape[2])
    w_gate_full, w_up_full, w_down_full, w_out_full = gather_packed(
        [w_gate, w_up, w_down, w_out], [0, 0, 1, 1], "req"
    )
    width = w_qkv.shape[2]
    heads_local = width // HD
    slots = k_cache.shape[1]
    full_rows = lax.all_gather(hidden_in, "mp", axis=1, tiled=True)
    normed = rms_scale(full_rows, attn_gain)
    blocks = normed.reshape(new_count, side, side, -1)
    columns = jnp.roll(blocks, (-row, -col), axis=(1, 2)).reshape(new_count, -1)
    projected = jnp.einsum(
        "nd,kdw->knw",
        columns,
        w_qkv_full,
        preferred_element_type=jnp.float32,
    )
    length = cache_len[0]
    positions = (length + jnp.arange(new_count, dtype=jnp.int32)).astype(jnp.float32)
    half = HD // 2
    lane = jnp.arange(width, dtype=jnp.int32)
    within = lane % HD
    partner_lane = lane - within + (within + half) % HD
    swap = (lane[:, None] == partner_lane[None, :]).astype(jnp.float32)
    partner = jnp.einsum(
        "knw,wv->knv", projected[:2], swap, precision=lax.Precision.HIGHEST,
        preferred_element_type=jnp.float32,
    )
    freq = THETA ** (-((within % half).astype(jnp.float32) * 2.0 / HD))
    angle = positions[:, None] * freq[None, :]
    cosine = jnp.cos(angle)
    sine = jnp.where(within < half, -1.0, 1.0)[None, :] * jnp.sin(angle)
    queries = (projected[0] * cosine + partner[0] * sine).astype(jnp.bfloat16).reshape(
        new_count, heads_local, HD
    )
    fresh_keys = (projected[1] * cosine + partner[1] * sine).astype(jnp.bfloat16).reshape(
        new_count, heads_local, HD
    )
    fresh_values = projected[2].astype(jnp.bfloat16).reshape(new_count, heads_local, HD)
    attn = flash_attention(
        cache_len,
        queries.reshape(new_count, width),
        k_cache[0],
        v_cache[0],
        fresh_keys.reshape(new_count, width),
        fresh_values.reshape(new_count, width),
    )
    partial_value = jnp.dot(
        attn, w_out_full, preferred_element_type=jnp.float32
    )
    summed = lax.psum(partial_value.astype(jnp.bfloat16), "mp").astype(jnp.float32)
    mid_full = (full_rows.astype(jnp.float32) + summed).astype(jnp.bfloat16)
    own = hidden_in.shape[1]
    mid_local = lax.dynamic_slice_in_dim(mid_full, lax.axis_index("mp") * own, own, axis=1)
    normed2 = rms_scale(mid_full, mlp_gain)
    columns = normed2
    gate = jnp.dot(
        columns,
        w_gate_full,
        preferred_element_type=jnp.float32,
    )
    upper = jnp.dot(
        columns, w_up_full, preferred_element_type=jnp.float32
    )
    units = (jax.nn.silu(gate) * upper).astype(jnp.bfloat16)
    terms = jnp.dot(
        units, w_down_full, preferred_element_type=jnp.float32
    )
    reduced = lax.psum_scatter(
        terms.astype(jnp.bfloat16), "mp", scatter_dimension=1, tiled=True
    ).astype(jnp.float32)
    hidden_out = (mid_local.astype(jnp.float32) + reduced).astype(jnp.bfloat16)
    return (
        hidden_out,
        fresh_keys.reshape(new_count, width),
        fresh_values.reshape(new_count, width),
    )


def solution(mesh):
    return jax.shard_map(
        on_device,
        mesh=mesh,
        in_specs=(
            P("req", "mp"),
            P(None, "req", "mp"),
            P("mp", "req"),
            P(),
            P(),
            P("req", "mp"),
            P("req", "mp"),
            P("mp", "req"),
            P("req", None, "mp"),
            P("req", None, "mp"),
            P("req"),
        ),
        out_specs=(P("req", "mp"), P("req", "mp"), P("req", "mp")),
        check_vma=False,
    )
```

```python
import jax
import jax.numpy as jnp
from jax import lax
from jax.sharding import PartitionSpec as P
from jax.experimental import pallas as pl
from jax.experimental.pallas import tpu as pltpu
import functools

HD = 64


THETA = 130000.0
EPSILON = 1e-05
NEG_FILL = -1e30


def rms_scale(rows, gain):
    values = rows.astype(jnp.float32)
    meansq = jnp.mean(values * values, axis=-1, keepdims=True)
    return (values * lax.rsqrt(meansq + EPSILON) * gain.astype(jnp.float32)).astype(jnp.bfloat16)


def gather_req_shifted(block, axis, axis_name):
    count = lax.axis_size(axis_name)
    side = int(round(count ** 0.5))
    me = lax.axis_index(axis_name)
    row, col = me // side, me % side

    def inner(k):
        return [(s, (s // side) * side + (s % side - k) % side) for s in range(count)]

    def outer(k):
        return [(s, ((s // side - k) % side) * side + s % side) for s in range(count)]

    parts = [block] + [lax.ppermute(block, axis_name, inner(k)) for k in range(1, side)]
    stage = jnp.stack(parts, axis=axis)
    parts = [stage] + [lax.ppermute(stage, axis_name, outer(k)) for k in range(1, side)]
    return jnp.stack(parts, axis=axis), row, col


def gather_packed(blocks, axes, axis_name):
    count = lax.axis_size(axis_name)
    lane = 128
    joined = jnp.concatenate([block.reshape(-1, lane) for block in blocks], axis=0)
    gathered = lax.all_gather(joined, axis_name, axis=0, tiled=False)
    outs = []
    offset = 0
    for block, axis in zip(blocks, axes):
        rows = block.size // lane
        piece = gathered[:, offset:offset + rows].reshape((count,) + block.shape)
        piece = jnp.moveaxis(piece, 0, axis)
        shape = list(block.shape)
        shape[axis] *= count
        outs.append(piece.reshape(shape))
        offset += rows
    return outs


def flash_body(len_ref, q_ref, kc_ref, vc_ref, kn_ref, vn_ref, o_ref, m_sc, l_sc, acc_sc, *, tk, n_cache, scale):
    j = pl.program_id(1)
    length = len_ref[0]
    tq = q_ref.shape[0]
    pair = q_ref.shape[1] // HD

    @pl.when(j == 0)
    def _():
        m_sc[...] = jnp.full(m_sc.shape, NEG_FILL, jnp.float32)
        l_sc[...] = jnp.zeros(l_sc.shape, jnp.float32)
        acc_sc[...] = jnp.zeros(acc_sc.shape, jnp.float32)

    def update(keys_of, values_of, mask):
        for head in range(pair):
            lanes = pl.ds(head * HD, HD)
            q = q_ref[:, lanes] * scale
            s = lax.dot_general(q, keys_of(lanes), (((1,), (1,)), ((), ())), preferred_element_type=jnp.float32)
            if mask is not None:
                s = jnp.where(mask, s, NEG_FILL)
            m_prev = m_sc[head]
            m_new = jnp.maximum(m_prev, jnp.max(s, axis=1, keepdims=True))
            alpha = jnp.exp(m_prev - m_new)
            p = jnp.exp(s - m_new)
            if mask is not None:
                p = jnp.where(mask, p, 0.0)
            l_sc[head] = alpha * l_sc[head] + jnp.sum(p, axis=1, keepdims=True)
            acc_sc[head] = alpha * acc_sc[head] + jnp.dot(
                p.astype(jnp.bfloat16), values_of(lanes), preferred_element_type=jnp.float32
            )
            m_sc[head] = m_new

    begin = j * tk
    in_cache = j < n_cache

    @pl.when(jnp.logical_not(in_cache) | (begin < length))
    def _():
        row = lax.broadcasted_iota(jnp.int32, (tq, tk), 0)
        col = lax.broadcasted_iota(jnp.int32, (tq, tk), 1)
        mask = col < jnp.where(in_cache, length - begin, row + 1)
        update(
            lambda lanes: jnp.where(in_cache, kc_ref[:, lanes], kn_ref[:, lanes]),
            lambda lanes: jnp.where(in_cache, vc_ref[:, lanes], vn_ref[:, lanes]),
            mask,
        )

    @pl.when(j == n_cache)
    def _():
        for head in range(pair):
            o_ref[:, pl.ds(head * HD, HD)] = (acc_sc[head] / l_sc[head]).astype(o_ref.dtype)


def flash_attention(length, q, kc, vc, kn, vn):
    new_count, width = q.shape
    slots = kc.shape[0]
    tk = min(new_count, slots)
    n_cache = slots // tk
    lanes = 2 * HD if width % (2 * HD) == 0 else width
    pair = lanes // HD
    body = functools.partial(flash_body, tk=tk, n_cache=n_cache, scale=HD ** (-0.5))

    def cache_map(h, j, len_ref):
        last = jnp.maximum(len_ref[0] - 1, 0) // tk
        return (jnp.minimum(j, last), h)

    fixed = lambda h, j, len_ref: (0, h)
    grid_spec = pltpu.PrefetchScalarGridSpec(
        num_scalar_prefetch=1,
        grid=(width // lanes, n_cache + 1),
        in_specs=[
            pl.BlockSpec((new_count, lanes), fixed),
            pl.BlockSpec((tk, lanes), cache_map),
            pl.BlockSpec((tk, lanes), cache_map),
            pl.BlockSpec((new_count, lanes), fixed),
            pl.BlockSpec((new_count, lanes), fixed),
        ],
        out_specs=pl.BlockSpec((new_count, lanes), fixed),
        scratch_shapes=[
            pltpu.VMEM((pair, new_count, 1), jnp.float32),
            pltpu.VMEM((pair, new_count, 1), jnp.float32),
            pltpu.VMEM((pair, new_count, HD), jnp.float32),
        ],
    )
    heads = width // HD
    cost = pl.CostEstimate(
        flops=4 * heads * new_count * (slots + new_count) * HD,
        transcendentals=heads * new_count * (slots + new_count),
        bytes_accessed=2 * (q.size + kc.size + vc.size + kn.size + vn.size) + 2 * q.size,
    )
    return pl.pallas_call(
        body,
        grid_spec=grid_spec,
        out_shape=jax.ShapeDtypeStruct((new_count, width), jnp.bfloat16),
        compiler_params=pltpu.CompilerParams(
            dimension_semantics=("arbitrary", "arbitrary"), vmem_limit_bytes=56 * 1024 * 1024
        ),
        cost_estimate=cost,
    )(length, q, kc, vc, kn, vn)


def on_device(
    hidden_in, w_qkv, w_out, attn_gain, mlp_gain, w_gate, w_up, w_down, k_cache, v_cache, cache_len
):
    new_count = hidden_in.shape[0]
    qkv_shifted, row, col = gather_req_shifted(w_qkv, 1, "req")
    side = qkv_shifted.shape[1]
    w_qkv_full = qkv_shifted.reshape(3, -1, w_qkv.shape[2])
    w_gate_full, w_up_full, w_down_full, w_out_full = gather_packed(
        [w_gate, w_up, w_down, w_out], [0, 0, 1, 1], "req"
    )
    width = w_qkv.shape[2]
    heads_local = width // HD
    slots = k_cache.shape[1]
    n_mp = lax.axis_size("mp")
    chips = n_mp // 2
    mine = lax.axis_index("mp")
    chip, core = mine // 2, mine % 2
    pair_perm = [(s, s ^ 1) for s in range(n_mp)]
    remote = [
        lax.ppermute(hidden_in, "mp", [(s, (s - 2 * dx) % n_mp) for s in range(n_mp)])
        for dx in range(1, chips)
    ]
    sibling = lax.ppermute(hidden_in, "mp", pair_perm)
    sibling_remote = lax.ppermute(jnp.stack(remote), "mp", pair_perm)
    pieces = [hidden_in, sibling]
    for dx in range(chips - 1):
        pieces += [remote[dx], sibling_remote[dx]]
    lane = 128
    per_piece = hidden_in.shape[1] // lane
    held = jnp.concatenate([piece.reshape(new_count, per_piece, lane) for piece in pieces], axis=1)

    def held_index(block):
        owner = block // per_piece
        return (((owner // 2 - chip) % chips) * 2 + (owner % 2 ^ core)) * per_piece + block % per_piece

    n_blocks = side * side
    order = jnp.arange(n_blocks, dtype=jnp.int32)
    wanted = ((row + order // side) % side) * side + (col + order % side) % side
    hidden_cols = jnp.take(held, held_index(wanted), axis=1).reshape(new_count, -1)
    gain_cols = jnp.take(attn_gain.reshape(n_blocks, lane), wanted, axis=0).reshape(-1)
    columns = rms_scale(hidden_cols, gain_cols)
    full_rows = jnp.take(held, held_index(order), axis=1).reshape(new_count, -1)
    projected = jnp.einsum(
        "nd,kdw->knw",
        columns,
        w_qkv_full,
        preferred_element_type=jnp.float32,
    )
    length = cache_len[0]
    positions = (length + jnp.arange(new_count, dtype=jnp.int32)).astype(jnp.float32)
    half = HD // 2
    lane = jnp.arange(width, dtype=jnp.int32)
    within = lane % HD
    partner_lane = lane - within + (within + half) % HD
    swap = (lane[:, None] == partner_lane[None, :]).astype(jnp.float32)
    partner = jnp.einsum(
        "knw,wv->knv", projected[:2], swap, precision=lax.Precision.HIGHEST,
        preferred_element_type=jnp.float32,
    )
    freq = THETA ** (-((within % half).astype(jnp.float32) * 2.0 / HD))
    angle = positions[:, None] * freq[None, :]
    cosine = jnp.cos(angle)
    sine = jnp.where(within < half, -1.0, 1.0)[None, :] * jnp.sin(angle)
    queries = (projected[0] * cosine + partner[0] * sine).astype(jnp.bfloat16).reshape(
        new_count, heads_local, HD
    )
    fresh_keys = (projected[1] * cosine + partner[1] * sine).astype(jnp.bfloat16).reshape(
        new_count, heads_local, HD
    )
    fresh_values = projected[2].astype(jnp.bfloat16).reshape(new_count, heads_local, HD)
    attn = flash_attention(
        cache_len,
        queries.reshape(new_count, width),
        k_cache[0],
        v_cache[0],
        fresh_keys.reshape(new_count, width),
        fresh_values.reshape(new_count, width),
    )
    partial_value = jnp.dot(
        attn, w_out_full, preferred_element_type=jnp.float32
    )
    summed = lax.psum(partial_value.astype(jnp.bfloat16), "mp").astype(jnp.float32)
    mid_full = (full_rows.astype(jnp.float32) + summed).astype(jnp.bfloat16)
    own = hidden_in.shape[1]
    mid_local = lax.dynamic_slice_in_dim(mid_full, lax.axis_index("mp") * own, own, axis=1)
    normed2 = rms_scale(mid_full, mlp_gain)
    columns = normed2
    gate = jnp.dot(
        columns,
        w_gate_full,
        preferred_element_type=jnp.float32,
    )
    upper = jnp.dot(
        columns, w_up_full, preferred_element_type=jnp.float32
    )
    units = (jax.nn.silu(gate) * upper).astype(jnp.bfloat16)
    terms = jnp.dot(
        units, w_down_full, preferred_element_type=jnp.float32
    )
    reduced = lax.psum_scatter(
        terms.astype(jnp.bfloat16), "mp", scatter_dimension=1, tiled=True
    ).astype(jnp.float32)
    hidden_out = (mid_local.astype(jnp.float32) + reduced).astype(jnp.bfloat16)
    return (
        hidden_out,
        fresh_keys.reshape(new_count, width),
        fresh_values.reshape(new_count, width),
    )


def solution(mesh):
    return jax.shard_map(
        on_device,
        mesh=mesh,
        in_specs=(
            P("req", "mp"),
            P(None, "req", "mp"),
            P("mp", "req"),
            P(),
            P(),
            P("req", "mp"),
            P("req", "mp"),
            P("mp", "req"),
            P("req", None, "mp"),
            P("req", None, "mp"),
            P("req"),
        ),
        out_specs=(P("req", "mp"), P("req", "mp"), P("req", "mp")),
        check_vma=False,
    )
```

```python
import jax
import jax.numpy as jnp
from jax import lax
from jax.sharding import PartitionSpec as P
from jax.experimental import pallas as pl
from jax.experimental.pallas import tpu as pltpu
import functools

HD = 64


THETA = 130000.0
EPSILON = 1e-05
NEG_FILL = -1e30


def rms_scale(rows, gain):
    values = rows.astype(jnp.float32)
    meansq = jnp.mean(values * values, axis=-1, keepdims=True)
    return (values * lax.rsqrt(meansq + EPSILON) * gain.astype(jnp.float32)).astype(jnp.bfloat16)


def gather_req_shifted(block, axis, axis_name):
    count = lax.axis_size(axis_name)
    side = int(round(count ** 0.5))
    me = lax.axis_index(axis_name)
    row, col = me // side, me % side

    def inner(k):
        return [(s, (s // side) * side + (s % side - k) % side) for s in range(count)]

    def outer(k):
        return [(s, ((s // side - k) % side) * side + s % side) for s in range(count)]

    parts = [block] + [lax.ppermute(block, axis_name, inner(k)) for k in range(1, side)]
    stage = jnp.stack(parts, axis=axis)
    parts = [stage] + [lax.ppermute(stage, axis_name, outer(k)) for k in range(1, side)]
    return jnp.stack(parts, axis=axis), row, col


def gather_packed(blocks, axes, axis_name):
    count = lax.axis_size(axis_name)
    lane = 128
    joined = jnp.concatenate([block.reshape(-1, lane) for block in blocks], axis=0)
    gathered = lax.all_gather(joined, axis_name, axis=0, tiled=False)
    outs = []
    offset = 0
    for block, axis in zip(blocks, axes):
        rows = block.size // lane
        piece = gathered[:, offset:offset + rows].reshape((count,) + block.shape)
        piece = jnp.moveaxis(piece, 0, axis)
        shape = list(block.shape)
        shape[axis] *= count
        outs.append(piece.reshape(shape))
        offset += rows
    return outs


def flash_body(len_ref, q_ref, kc_ref, vc_ref, kn_ref, vn_ref, o_ref, m_sc, l_sc, acc_sc, *, tk, n_cache, scale):
    j = pl.program_id(1)
    length = len_ref[0]
    tq = q_ref.shape[0]
    pair = q_ref.shape[1] // HD

    @pl.when(j == 0)
    def _():
        m_sc[...] = jnp.full(m_sc.shape, NEG_FILL, jnp.float32)
        l_sc[...] = jnp.zeros(l_sc.shape, jnp.float32)
        acc_sc[...] = jnp.zeros(acc_sc.shape, jnp.float32)

    def update(k_ref, v_ref, mask):
        for head in range(pair):
            lanes = pl.ds(head * HD, HD)
            q = q_ref[:, lanes] * scale
            s = lax.dot_general(q, k_ref[:, lanes], (((1,), (1,)), ((), ())), preferred_element_type=jnp.float32)
            if mask is not None:
                s = jnp.where(mask, s, NEG_FILL)
            m_prev = m_sc[head]
            m_new = jnp.maximum(m_prev, jnp.max(s, axis=1, keepdims=True))
            alpha = jnp.exp(m_prev - m_new)
            p = jnp.exp(s - m_new)
            if mask is not None:
                p = jnp.where(mask, p, 0.0)
            l_sc[head] = alpha * l_sc[head] + jnp.sum(p, axis=1, keepdims=True)
            acc_sc[head] = alpha * acc_sc[head] + jnp.dot(
                p.astype(jnp.bfloat16), v_ref[:, lanes], preferred_element_type=jnp.float32
            )
            m_sc[head] = m_new

    begin = j * tk

    @pl.when((j < n_cache) & (begin + tk <= length))
    def _():
        update(kc_ref, vc_ref, None)

    @pl.when((j < n_cache) & (begin < length) & (begin + tk > length))
    def _():
        col = begin + lax.broadcasted_iota(jnp.int32, (tq, tk), 1)
        update(kc_ref, vc_ref, col < length)

    @pl.when(j == n_cache)
    def _():
        row = lax.broadcasted_iota(jnp.int32, (tq, tq), 0)
        col = lax.broadcasted_iota(jnp.int32, (tq, tq), 1)
        update(kn_ref, vn_ref, row >= col)
        for head in range(pair):
            o_ref[:, pl.ds(head * HD, HD)] = (acc_sc[head] / l_sc[head]).astype(o_ref.dtype)


def flash_attention(length, q, kc, vc, kn, vn):
    new_count, width = q.shape
    slots = kc.shape[0]
    tk = min(new_count, slots)
    n_cache = slots // tk
    lanes = 2 * HD if width % (2 * HD) == 0 else width
    pair = lanes // HD
    body = functools.partial(flash_body, tk=tk, n_cache=n_cache, scale=HD ** (-0.5))

    def cache_map(h, j, len_ref):
        last = jnp.maximum(len_ref[0] - 1, 0) // tk
        return (jnp.minimum(j, last), h)

    fixed = lambda h, j, len_ref: (0, h)
    grid_spec = pltpu.PrefetchScalarGridSpec(
        num_scalar_prefetch=1,
        grid=(width // lanes, n_cache + 1),
        in_specs=[
            pl.BlockSpec((new_count, lanes), fixed),
            pl.BlockSpec((tk, lanes), cache_map),
            pl.BlockSpec((tk, lanes), cache_map),
            pl.BlockSpec((new_count, lanes), fixed),
            pl.BlockSpec((new_count, lanes), fixed),
        ],
        out_specs=pl.BlockSpec((new_count, lanes), fixed),
        scratch_shapes=[
            pltpu.VMEM((pair, new_count, 1), jnp.float32),
            pltpu.VMEM((pair, new_count, 1), jnp.float32),
            pltpu.VMEM((pair, new_count, HD), jnp.float32),
        ],
    )
    heads = width // HD
    cost = pl.CostEstimate(
        flops=4 * heads * new_count * (slots + new_count) * HD,
        transcendentals=heads * new_count * (slots + new_count),
        bytes_accessed=2 * (q.size + kc.size + vc.size + kn.size + vn.size) + 2 * q.size,
    )
    return pl.pallas_call(
        body,
        grid_spec=grid_spec,
        out_shape=jax.ShapeDtypeStruct((new_count, width), jnp.bfloat16),
        compiler_params=pltpu.CompilerParams(
            dimension_semantics=("arbitrary", "arbitrary"), vmem_limit_bytes=56 * 1024 * 1024
        ),
        cost_estimate=cost,
    )(length, q, kc, vc, kn, vn)


def on_device(
    hidden_in, w_qkv, w_out, attn_gain, mlp_gain, w_gate, w_up, w_down, k_cache, v_cache, cache_len
):
    new_count = hidden_in.shape[0]
    qkv_shifted, row, col = gather_req_shifted(w_qkv, 1, "req")
    side = qkv_shifted.shape[1]
    w_qkv_full = qkv_shifted.reshape(3, -1, w_qkv.shape[2])
    out_shifted, _, _ = gather_req_shifted(w_out, 1, "req")
    w_out_full = jnp.roll(out_shifted, (row, col), axis=(1, 2)).reshape(w_out.shape[0], -1)
    w_gate_full, w_up_full, w_down_full = gather_packed([w_gate, w_up, w_down], [0, 0, 1], "req")
    width = w_qkv.shape[2]
    heads_local = width // HD
    slots = k_cache.shape[1]
    full_rows = lax.all_gather(hidden_in, "mp", axis=1, tiled=True)
    normed = rms_scale(full_rows, attn_gain)
    blocks = normed.reshape(new_count, side, side, -1)
    columns = jnp.roll(blocks, (-row, -col), axis=(1, 2)).reshape(new_count, -1)
    projected = jnp.einsum(
        "nd,kdw->knw",
        columns,
        w_qkv_full,
        preferred_element_type=jnp.float32,
    )
    length = cache_len[0]
    positions = (length + jnp.arange(new_count, dtype=jnp.int32)).astype(jnp.float32)
    half = HD // 2
    lane = jnp.arange(width, dtype=jnp.int32)
    within = lane % HD
    partner_lane = lane - within + (within + half) % HD
    swap = (lane[:, None] == partner_lane[None, :]).astype(jnp.float32)
    partner = jnp.einsum(
        "knw,wv->knv", projected[:2], swap, precision=lax.Precision.HIGHEST,
        preferred_element_type=jnp.float32,
    )
    freq = THETA ** (-((within % half).astype(jnp.float32) * 2.0 / HD))
    angle = positions[:, None] * freq[None, :]
    cosine = jnp.cos(angle)
    sine = jnp.where(within < half, -1.0, 1.0)[None, :] * jnp.sin(angle)
    queries = (projected[0] * cosine + partner[0] * sine).astype(jnp.bfloat16).reshape(
        new_count, heads_local, HD
    )
    fresh_keys = (projected[1] * cosine + partner[1] * sine).astype(jnp.bfloat16).reshape(
        new_count, heads_local, HD
    )
    fresh_values = projected[2].astype(jnp.bfloat16).reshape(new_count, heads_local, HD)
    attn = flash_attention(
        cache_len,
        queries.reshape(new_count, width),
        k_cache[0],
        v_cache[0],
        fresh_keys.reshape(new_count, width),
        fresh_values.reshape(new_count, width),
    )
    partial_value = jnp.dot(
        attn, w_out_full, preferred_element_type=jnp.float32
    )
    after_pack = (w_gate_full[0, 0] * 0).astype(jnp.bfloat16)
    summed = lax.psum(partial_value.astype(jnp.bfloat16) + after_pack, "mp").astype(jnp.float32)
    mid_full = (full_rows.astype(jnp.float32) + summed).astype(jnp.bfloat16)
    own = hidden_in.shape[1]
    mid_local = lax.dynamic_slice_in_dim(mid_full, lax.axis_index("mp") * own, own, axis=1)
    normed2 = rms_scale(mid_full, mlp_gain)
    columns = normed2
    gate = jnp.dot(
        columns,
        w_gate_full,
        preferred_element_type=jnp.float32,
    )
    upper = jnp.dot(
        columns, w_up_full, preferred_element_type=jnp.float32
    )
    units = (jax.nn.silu(gate) * upper).astype(jnp.bfloat16)
    terms = jnp.dot(
        units, w_down_full, preferred_element_type=jnp.float32
    )
    reduced = lax.psum_scatter(
        terms.astype(jnp.bfloat16), "mp", scatter_dimension=1, tiled=True
    ).astype(jnp.float32)
    hidden_out = (mid_local.astype(jnp.float32) + reduced).astype(jnp.bfloat16)
    return (
        hidden_out,
        fresh_keys.reshape(new_count, width),
        fresh_values.reshape(new_count, width),
    )


def solution(mesh):
    return jax.shard_map(
        on_device,
        mesh=mesh,
        in_specs=(
            P("req", "mp"),
            P(None, "req", "mp"),
            P("mp", "req"),
            P(),
            P(),
            P("req", "mp"),
            P("req", "mp"),
            P("mp", "req"),
            P("req", None, "mp"),
            P("req", None, "mp"),
            P("req"),
        ),
        out_specs=(P("req", "mp"), P("req", "mp"), P("req", "mp")),
        check_vma=False,
    )
```

```python
import jax
import jax.numpy as jnp
from jax import lax
from jax.sharding import PartitionSpec as P
from jax.experimental import pallas as pl
from jax.experimental.pallas import tpu as pltpu
import functools

HD = 64


THETA = 130000.0
EPSILON = 1e-05
NEG_FILL = -1e30


def rms_scale(rows, gain):
    values = rows.astype(jnp.float32)
    meansq = jnp.mean(values * values, axis=-1, keepdims=True)
    return (values * lax.rsqrt(meansq + EPSILON) * gain.astype(jnp.float32)).astype(jnp.bfloat16)


def gather_req_shifted(block, axis, axis_name):
    count = lax.axis_size(axis_name)
    side = int(round(count ** 0.5))
    me = lax.axis_index(axis_name)
    row, col = me // side, me % side

    def inner(k):
        return [(s, (s // side) * side + (s % side - k) % side) for s in range(count)]

    def outer(k):
        return [(s, ((s // side - k) % side) * side + s % side) for s in range(count)]

    parts = [block] + [lax.ppermute(block, axis_name, inner(k)) for k in range(1, side)]
    stage = jnp.stack(parts, axis=axis)
    parts = [stage] + [lax.ppermute(stage, axis_name, outer(k)) for k in range(1, side)]
    return jnp.stack(parts, axis=axis), row, col


def gather_packed(blocks, axes, axis_name):
    count = lax.axis_size(axis_name)
    lane = 128
    joined = jnp.concatenate([block.reshape(-1, lane) for block in blocks], axis=0)
    gathered = lax.all_gather(joined, axis_name, axis=0, tiled=False)
    outs = []
    offset = 0
    for block, axis in zip(blocks, axes):
        rows = block.size // lane
        piece = gathered[:, offset:offset + rows].reshape((count,) + block.shape)
        piece = jnp.moveaxis(piece, 0, axis)
        shape = list(block.shape)
        shape[axis] *= count
        outs.append(piece.reshape(shape))
        offset += rows
    return outs


def flash_body(len_ref, q_ref, kc_ref, vc_ref, kn_ref, vn_ref, o_ref, m_sc, l_sc, acc_sc, *, tk, n_cache, scale):
    j = pl.program_id(1)
    length = len_ref[0]
    tq = q_ref.shape[0]
    pair = q_ref.shape[1] // HD

    @pl.when(j == 0)
    def _():
        m_sc[...] = jnp.full(m_sc.shape, NEG_FILL, jnp.float32)
        l_sc[...] = jnp.zeros(l_sc.shape, jnp.float32)
        acc_sc[...] = jnp.zeros(acc_sc.shape, jnp.float32)

    def update(keys_of, values_of, mask):
        for head in range(pair):
            lanes = pl.ds(head * HD, HD)
            q = q_ref[:, lanes] * scale
            s = lax.dot_general(q, keys_of(lanes), (((1,), (1,)), ((), ())), preferred_element_type=jnp.float32)
            if mask is not None:
                s = jnp.where(mask, s, NEG_FILL)
            m_prev = m_sc[head]
            m_new = jnp.maximum(m_prev, jnp.max(s, axis=1, keepdims=True))
            alpha = jnp.exp(m_prev - m_new)
            p = jnp.exp(s - m_new)
            if mask is not None:
                p = jnp.where(mask, p, 0.0)
            l_sc[head] = alpha * l_sc[head] + jnp.sum(p, axis=1, keepdims=True)
            acc_sc[head] = alpha * acc_sc[head] + jnp.dot(
                p.astype(jnp.bfloat16), values_of(lanes), preferred_element_type=jnp.float32
            )
            m_sc[head] = m_new

    begin = j * tk
    in_cache = j < n_cache

    @pl.when(jnp.logical_not(in_cache) | (begin < length))
    def _():
        row = lax.broadcasted_iota(jnp.int32, (tq, tk), 0)
        col = lax.broadcasted_iota(jnp.int32, (tq, tk), 1)
        mask = col < jnp.where(in_cache, length - begin, row + 1)
        update(
            lambda lanes: jnp.where(in_cache, kc_ref[:, lanes], kn_ref[:, lanes]),
            lambda lanes: jnp.where(in_cache, vc_ref[:, lanes], vn_ref[:, lanes]),
            mask,
        )

    @pl.when(j == n_cache)
    def _():
        for head in range(pair):
            o_ref[:, pl.ds(head * HD, HD)] = (acc_sc[head] / l_sc[head]).astype(o_ref.dtype)


def flash_attention(length, q, kc, vc, kn, vn):
    new_count, width = q.shape
    slots = kc.shape[0]
    tk = min(new_count, slots)
    n_cache = slots // tk
    lanes = 2 * HD if width % (2 * HD) == 0 else width
    pair = lanes // HD
    body = functools.partial(flash_body, tk=tk, n_cache=n_cache, scale=HD ** (-0.5))

    def cache_map(h, j, len_ref):
        last = jnp.maximum(len_ref[0] - 1, 0) // tk
        return (jnp.minimum(j, last), h)

    fixed = lambda h, j, len_ref: (0, h)
    grid_spec = pltpu.PrefetchScalarGridSpec(
        num_scalar_prefetch=1,
        grid=(width // lanes, n_cache + 1),
        in_specs=[
            pl.BlockSpec((new_count, lanes), fixed),
            pl.BlockSpec((tk, lanes), cache_map),
            pl.BlockSpec((tk, lanes), cache_map),
            pl.BlockSpec((new_count, lanes), fixed),
            pl.BlockSpec((new_count, lanes), fixed),
        ],
        out_specs=pl.BlockSpec((new_count, lanes), fixed),
        scratch_shapes=[
            pltpu.VMEM((pair, new_count, 1), jnp.float32),
            pltpu.VMEM((pair, new_count, 1), jnp.float32),
            pltpu.VMEM((pair, new_count, HD), jnp.float32),
        ],
    )
    heads = width // HD
    cost = pl.CostEstimate(
        flops=4 * heads * new_count * (slots + new_count) * HD,
        transcendentals=heads * new_count * (slots + new_count),
        bytes_accessed=2 * (q.size + kc.size + vc.size + kn.size + vn.size) + 2 * q.size,
    )
    return pl.pallas_call(
        body,
        grid_spec=grid_spec,
        out_shape=jax.ShapeDtypeStruct((new_count, width), jnp.bfloat16),
        compiler_params=pltpu.CompilerParams(
            dimension_semantics=("arbitrary", "arbitrary"), vmem_limit_bytes=56 * 1024 * 1024
        ),
        cost_estimate=cost,
    )(length, q, kc, vc, kn, vn)


def on_device(
    hidden_in, w_qkv, w_out, attn_gain, mlp_gain, w_gate, w_up, w_down, k_cache, v_cache, cache_len
):
    new_count = hidden_in.shape[0]
    qkv_shifted, row, col = gather_req_shifted(w_qkv, 1, "req")
    side = qkv_shifted.shape[1]
    w_qkv_full = qkv_shifted.reshape(3, -1, w_qkv.shape[2])
    w_gate_full, w_up_full, w_down_full, w_out_full = gather_packed(
        [w_gate, w_up, w_down, w_out], [0, 0, 1, 1], "req"
    )
    width = w_qkv.shape[2]
    heads_local = width // HD
    slots = k_cache.shape[1]
    full_rows = lax.all_gather(hidden_in, "mp", axis=1, tiled=True)
    normed = rms_scale(full_rows, attn_gain)
    blocks = normed.reshape(new_count, side, side, -1)
    columns = jnp.roll(blocks, (-row, -col), axis=(1, 2)).reshape(new_count, -1)
    projected = jnp.einsum(
        "nd,kdw->knw",
        columns,
        w_qkv_full,
        preferred_element_type=jnp.float32,
    )
    length = cache_len[0]
    positions = (length + jnp.arange(new_count, dtype=jnp.int32)).astype(jnp.float32)
    half = HD // 2
    lane = jnp.arange(width, dtype=jnp.int32)
    within = lane % HD
    partner_lane = lane - within + (within + half) % HD
    swap = (lane[:, None] == partner_lane[None, :]).astype(jnp.float32)
    partner = jnp.einsum(
        "knw,wv->knv", projected[:2], swap, precision=lax.Precision.HIGHEST,
        preferred_element_type=jnp.float32,
    )
    freq = THETA ** (-((within % half).astype(jnp.float32) * 2.0 / HD))
    angle = positions[:, None] * freq[None, :]
    cosine = jnp.cos(angle)
    sine = jnp.where(within < half, -1.0, 1.0)[None, :] * jnp.sin(angle)
    queries = (projected[0] * cosine + partner[0] * sine).astype(jnp.bfloat16).reshape(
        new_count, heads_local, HD
    )
    fresh_keys = (projected[1] * cosine + partner[1] * sine).astype(jnp.bfloat16).reshape(
        new_count, heads_local, HD
    )
    fresh_values = projected[2].astype(jnp.bfloat16).reshape(new_count, heads_local, HD)
    attn = flash_attention(
        cache_len,
        queries.reshape(new_count, width),
        k_cache[0],
        v_cache[0],
        fresh_keys.reshape(new_count, width),
        fresh_values.reshape(new_count, width),
    )
    partial_value = jnp.dot(
        attn, w_out_full, preferred_element_type=jnp.float32
    )
    summed = lax.psum(partial_value.astype(jnp.bfloat16), "mp").astype(jnp.float32)
    mid_full = (full_rows.astype(jnp.float32) + summed).astype(jnp.bfloat16)
    own = hidden_in.shape[1]
    mid_local = lax.dynamic_slice_in_dim(mid_full, lax.axis_index("mp") * own, own, axis=1)
    normed2 = rms_scale(mid_full, mlp_gain)
    columns = normed2
    gate, upper = jnp.einsum(
        "nd,kdf->knf",
        columns,
        jnp.stack([w_gate_full, w_up_full]),
        preferred_element_type=jnp.float32,
    )
    units = (jax.nn.silu(gate) * upper).astype(jnp.bfloat16)
    terms = jnp.dot(
        units, w_down_full, preferred_element_type=jnp.float32
    )
    reduced = lax.psum_scatter(
        terms.astype(jnp.bfloat16), "mp", scatter_dimension=1, tiled=True
    ).astype(jnp.float32)
    hidden_out = (mid_local.astype(jnp.float32) + reduced).astype(jnp.bfloat16)
    return (
        hidden_out,
        fresh_keys.reshape(new_count, width),
        fresh_values.reshape(new_count, width),
    )


def solution(mesh):
    return jax.shard_map(
        on_device,
        mesh=mesh,
        in_specs=(
            P("req", "mp"),
            P(None, "req", "mp"),
            P("mp", "req"),
            P(),
            P(),
            P("req", "mp"),
            P("req", "mp"),
            P("mp", "req"),
            P("req", None, "mp"),
            P("req", None, "mp"),
            P("req"),
        ),
        out_specs=(P("req", "mp"), P("req", "mp"), P("req", "mp")),
        check_vma=False,
    )
```
